256 devices in a mesh: chain: 8 (over x, core), rows: 32 (over z, y).
Axes of the slice: x: 4, y: 4, z: 8, core: 2. Of those that a mesh axis runs over, the one named last changes fastest.
Arguments:
- right_spike: float32 [524288, 256], P(('chain', 'rows')), may hold values from -6 to 6
- left_spike: float32 [524288, 256], P(('chain', 'rows')), may hold values from -6 to 6
- loads: float32 [524288, 256], P(('chain', 'rows')), may hold values from -6 to 6
- tip_inverse: float32 [8, 3, 256, 512], P('chain'), may hold values from -0.0234375 to 0.0234375
Outputs:
- right_final: float32 [524288, 256], P(('chain', 'rows'))
- left_final: float32 [524288, 256], P(('chain', 'rows'))
- loads_final: float32 [524288, 256], P(('chain', 'rows'))
The draws below stay inside these ranges and needn't reach their ends.
All inputs are finite; a program needn't handle non-finite values.
Results may differ from the reference program's by a relative error of at most 0.00019.
Values sent between devices are 32-bit elements; how exact they have to be, the bound alone decides.
No kernel may reach another device: no remote copies, remote signals or barrier semaphores. Data moves between devices by JAX's collectives and lax.ppermute only.
A program may use at most 64 MiB of HBM per device.

```python
import jax
import jax.numpy as jnp
from jax import lax

HALF_BAND = 256
LOAD_COLS = 256
LEVELS = 3
SEGMENTS = 8
SEG_ROWS = 65536
ALL_ROWS = 524288


def steps_of(rng, dims, cuts, low, largest):
    factor_of = 1.0
    for dim, shards_of in cuts:
        steps = jax.random.uniform(jax.random.fold_in(jax.random.fold_in(rng, 6), dim), (shards_of,), jnp.float32, low / len(cuts), largest / len(cuts))
        factor_of = factor_of * jnp.repeat(jnp.exp(steps), dims[dim] // shards_of).reshape((-1,) + (1,) * (len(dims) - 1 - dim))
    return factor_of


def normal_values(rng, extent, scale, bound, cuts=(), held_as=jnp.bfloat16):
    values = jax.random.normal(rng, extent, jnp.float32) * scale
    if len(cuts) > 0:
        values = steps_of(rng, extent, cuts, -0.22, 0.18) * values
    return jnp.clip(values, min=-bound, max=bound).astype(held_as)


def setup_inputs(seed: int = 0) -> dict:
    arg_keys = jax.random.split(jax.random.key(seed), 5)
    return {
        "right_spike": normal_values(arg_keys[0], (ALL_ROWS, HALF_BAND), 1.0, 6.0, ((0, 256),), jnp.float32),
        "left_spike": normal_values(arg_keys[1], (ALL_ROWS, HALF_BAND), 1.0, 6.0, ((0, 256),), jnp.float32),
        "loads": normal_values(arg_keys[2], (ALL_ROWS, LOAD_COLS), 1.0, 6.0, ((0, 256),), jnp.float32),
        "tip_inverse": normal_values(arg_keys[3], (SEGMENTS, LEVELS, HALF_BAND, 2 * HALF_BAND), (HALF_BAND * HALF_BAND) ** -0.5, 0.0234375, ((0, 8),), jnp.float32),
    }


def reference(right_spike, left_spike, loads, tip_inverse):
    precise = lax.Precision.HIGHEST
    band = HALF_BAND
    width = LOAD_COLS
    spike_right = right_spike.reshape(SEGMENTS, SEG_ROWS, band)
    spike_left = left_spike.reshape(SEGMENTS, SEG_ROWS, band)
    load_block = loads.reshape(SEGMENTS, SEG_ROWS, width)
    for level in range(LEVELS):
        half = 2 ** level
        groups = SEGMENTS // (2 * half)
        right_five = spike_right.reshape(groups, 2, half, SEG_ROWS, band)
        left_five = spike_left.reshape(groups, 2, half, SEG_ROWS, band)
        load_five = load_block.reshape(groups, 2, half, SEG_ROWS, width)
        left_low = left_five[:, 0, half - 1, SEG_ROWS - band:, :]
        load_low = load_five[:, 0, half - 1, SEG_ROWS - band:, :]
        right_up = right_five[:, 1, 0, :band, :]
        load_up = load_five[:, 1, 0, :band, :]
        blank_block = jnp.zeros((groups, band, band), jnp.float32)
        upper_rows = jnp.concatenate([load_low, left_low, blank_block], 2)
        lower_rows = jnp.concatenate([load_up, blank_block, right_up], 2)
        tip_rhs = jnp.concatenate([upper_rows, lower_rows], 1)
        inverse_five = tip_inverse.reshape(groups, 2, half, LEVELS, band, 2 * band)
        inverse_first = inverse_five[:, 0, half - 1, level]
        inverse_second = inverse_five[:, 1, 0, level]
        solved_first = jnp.einsum("gij,gjc->gic", inverse_first, tip_rhs, precision=precise)
        solved_second = jnp.einsum("gij,gjc->gic", inverse_second, tip_rhs, precision=precise)
        prod_first = jnp.einsum("ghrb,gbc->ghrc", right_five[:, 0], solved_first, precision=precise)
        prod_second = jnp.einsum("ghrb,gbc->ghrc", left_five[:, 1], solved_second, precision=precise)
        load_first = load_five[:, 0] - prod_first[..., :width]
        load_second = load_five[:, 1] - prod_second[..., :width]
        left_first = left_five[:, 0] - prod_first[..., width:width + band]
        left_second = -prod_second[..., width:width + band]
        right_first = -prod_first[..., width + band:]
        right_second = right_five[:, 1] - prod_second[..., width + band:]
        spike_right = jnp.stack([right_first, right_second], 1).reshape(SEGMENTS, SEG_ROWS, band)
        spike_left = jnp.stack([left_first, left_second], 1).reshape(SEGMENTS, SEG_ROWS, band)
        load_block = jnp.stack([load_first, load_second], 1).reshape(SEGMENTS, SEG_ROWS, width)
    return (spike_right.reshape(ALL_ROWS, band), spike_left.reshape(ALL_ROWS, band), load_block.reshape(ALL_ROWS, width))
```

```python
import jax
import jax.numpy as jnp
from jax import lax
from jax.sharding import PartitionSpec as P

HALF_BAND = 256
LOAD_COLS = 256
LEVELS = 3


def partner_2(x, axis, distance):
    return lax.ppermute(x, axis, [(i, i ^ 1 << distance) for i in range(lax.axis_size(axis))])


def spread_block(block, level, chain_pos, side_low):
    source_bit = jnp.where(side_low, 1, 0)
    for bit in range(level):
        partner = partner_2(block, "chain", bit)
        own_bit = chain_pos // 2**bit % 2
        block = jnp.where(own_bit != source_bit, partner, block)
    return block


def spread_tips(top, bottom, row_pos, count):
    step = count // 2
    while step >= 1:
        pairs = [(s, s + step) for s in range(0, count, 2 * step)]
        pairs += [(s, s - step) for s in range(2 * step - 1, count, 2 * step)]
        sent = jnp.where(row_pos % (2 * step) == 0, top, bottom)
        got = lax.ppermute(sent, "rows", pairs)
        top = jnp.where(row_pos % (2 * step) == step, got, top)
        bottom = jnp.where(row_pos % (2 * step) == step - 1, got, bottom)
        step //= 2
    return top, bottom


def on_device(right_spike, left_spike, loads, tip_inverse):
    precise = lax.Precision.HIGHEST
    band = HALF_BAND
    width = LOAD_COLS
    chain_pos = lax.axis_index("chain")
    row_pos = lax.axis_index("rows")
    chain_count = lax.axis_size("chain")
    spike_right = right_spike
    spike_left = left_spike
    load_block = loads
    top, bottom = spread_tips(
        jnp.concatenate([load_block[:band], spike_right[:band]], 1),
        jnp.concatenate([load_block[-band:], spike_left[-band:]], 1),
        row_pos,
        lax.axis_size("rows"),
    )
    blank_block = jnp.zeros((band, band), jnp.float32)
    for level in range(LEVELS):
        half = 2**level
        place = chain_pos % (2 * half)
        side_low = place < half
        lasts = list(range(half - 1, chain_count - 1, 2 * half))
        next_top = lax.ppermute(top, "chain", [(a + 1, a) for a in lasts])
        prev_bottom = lax.ppermute(bottom, "chain", [(a, a + 1) for a in lasts])
        lower_tip = jnp.where(side_low, bottom, prev_bottom)
        upper_tip = jnp.where(side_low, next_top, top)
        upper_rows = jnp.concatenate([lower_tip[:, :band], lower_tip[:, band:], blank_block], 1)
        lower_rows = jnp.concatenate([upper_tip[:, :band], blank_block, upper_tip[:, band:]], 1)
        tip_rhs = jnp.concatenate([upper_rows, lower_rows], 0)
        solved = jnp.dot(
            tip_inverse[0, level], tip_rhs, precision=precise, preferred_element_type=jnp.float32
        )
        solved = spread_block(solved, level, chain_pos, side_low)
        if level + 1 < LEVELS:
            bottom_prod = jnp.dot(
                bottom[:, band:], solved[:, : 2 * band], precision=precise, preferred_element_type=jnp.float32
            )
            bottom = jnp.concatenate([bottom[:, :band] - bottom_prod[:, :band], -bottom_prod[:, band:]], 1)
            top_prod = jnp.dot(
                top[:, band:],
                jnp.concatenate([solved[:, :band], solved[:, 2 * band :]], 1),
                precision=precise,
                preferred_element_type=jnp.float32,
            )
            top = jnp.concatenate([top[:, :band] - top_prod[:, :band], -top_prod[:, band:]], 1)
        driver = jnp.where(side_low, spike_right, spike_left)
        product = jnp.dot(driver, solved, precision=precise, preferred_element_type=jnp.float32)
        left_term = product[:, width : width + band]
        right_term = product[:, width + band :]
        load_block = load_block - product[:, :width]
        new_left = jnp.where(side_low, spike_left - left_term, -left_term)
        new_right = jnp.where(side_low, -right_term, spike_right - right_term)
        spike_left = new_left
        spike_right = new_right
    return (spike_right, spike_left, load_block)


def solution(mesh):
    in_specs = (
        P(("chain", "rows"), None),
        P(("chain", "rows"), None),
        P(("chain", "rows"), None),
        P("chain", None, None, None),
    )
    out_specs = (P(("chain", "rows"), None), P(("chain", "rows"), None), P(("chain", "rows"), None))
    return jax.shard_map(
        on_device, mesh=mesh, in_specs=in_specs, out_specs=out_specs, check_vma=False
    )
```

```python
import jax
import jax.numpy as jnp
from jax import lax
from jax.sharding import PartitionSpec as P

HALF_BAND = 256
LOAD_COLS = 256
LEVELS = 3


def spread_tips(top, bottom, row_pos, count, fanouts):
    stride = count
    for fanout in fanouts:
        step = stride // fanout
        got_top = top
        got_bottom = bottom
        for k in range(1, fanout):
            offset = k * step
            pairs = [(s, s + offset) for s in range(0, count, stride)]
            pairs += [(s, s - offset) for s in range(stride - 1, count, stride)]
            sent = jnp.where(row_pos % stride == 0, top, bottom)
            got = lax.ppermute(sent, "rows", pairs)
            got_top = jnp.where(row_pos % stride == offset, got, got_top)
            got_bottom = jnp.where(row_pos % stride == stride - 1 - offset, got, got_bottom)
        top = got_top
        bottom = got_bottom
        stride = step
    return top, bottom


def row_fanouts(count):
    fanouts = []
    while count > 1:
        fanout = 4 if count % 4 == 0 else 2
        fanouts.append(fanout)
        count //= fanout
    return fanouts


def on_device(right_spike, left_spike, loads, tip_inverse):
    precise = lax.Precision.HIGHEST
    band = HALF_BAND
    width = LOAD_COLS
    chain_pos = lax.axis_index("chain")
    row_pos = lax.axis_index("rows")
    chain_count = lax.axis_size("chain")
    row_count = lax.axis_size("rows")
    spike_right = right_spike
    spike_left = left_spike
    load_block = loads
    inverses = [tip_inverse[0, 0]]
    for level in range(1, LEVELS):
        half = 2**level
        place = chain_pos % (2 * half)
        lasts = list(range(half - 1, chain_count - 1, 2 * half))
        mine = tip_inverse[0, level]
        for k in range(1, half):
            pairs = [(a, a - k) for a in lasts] + [(a + 1, a + 1 + k) for a in lasts]
            got = lax.ppermute(mine, "chain", pairs)
            mine = jnp.where((place == half - 1 - k) | (place == half + k), got, mine)
        inverses.append(mine)
    top, bottom = spread_tips(
        jnp.concatenate([load_block[:band], spike_right[:band]], 1),
        jnp.concatenate([load_block[-band:], spike_left[-band:]], 1),
        row_pos,
        row_count,
        row_fanouts(row_count),
    )
    blank_block = jnp.zeros((band, band), jnp.float32)
    for level in range(LEVELS):
        half = 2**level
        place = chain_pos % (2 * half)
        side_low = place < half
        lasts = list(range(half - 1, chain_count - 1, 2 * half))
        lower_tip = bottom
        upper_tip = top
        sent = jnp.where(place == half - 1, bottom, top)
        for offset in list(range(-(half - 1), 0)) + list(range(1, half + 1)):
            pairs = [(a, a + offset) for a in lasts] + [(a + 1, a + 1 - offset) for a in lasts]
            got = lax.ppermute(sent, "chain", pairs)
            lower_tip = jnp.where(place == half - 1 + offset, got, lower_tip)
            upper_tip = jnp.where(place == half - offset, got, upper_tip)
        upper_rows = jnp.concatenate([lower_tip[:, :band], lower_tip[:, band:], blank_block], 1)
        lower_rows = jnp.concatenate([upper_tip[:, :band], blank_block, upper_tip[:, band:]], 1)
        tip_rhs = jnp.concatenate([upper_rows, lower_rows], 0)
        solved = jnp.dot(inverses[level], tip_rhs, precision=precise, preferred_element_type=jnp.float32)
        if level + 1 < LEVELS:
            bottom_prod = jnp.dot(
                bottom[:, band:], solved[:, : 2 * band], precision=precise, preferred_element_type=jnp.float32
            )
            bottom = jnp.concatenate([bottom[:, :band] - bottom_prod[:, :band], -bottom_prod[:, band:]], 1)
            top_prod = jnp.dot(
                top[:, band:],
                jnp.concatenate([solved[:, :band], solved[:, 2 * band :]], 1),
                precision=precise,
                preferred_element_type=jnp.float32,
            )
            top = jnp.concatenate([top[:, :band] - top_prod[:, :band], -top_prod[:, band:]], 1)
        driver = jnp.where(side_low, spike_right, spike_left)
        product = jnp.dot(driver, solved, precision=precise, preferred_element_type=jnp.float32)
        left_term = product[:, width : width + band]
        right_term = product[:, width + band :]
        load_block = load_block - product[:, :width]
        new_left = jnp.where(side_low, spike_left - left_term, -left_term)
        new_right = jnp.where(side_low, -right_term, spike_right - right_term)
        spike_left = new_left
        spike_right = new_right
    return (spike_right, spike_left, load_block)


def solution(mesh):
    in_specs = (
        P(("chain", "rows"), None),
        P(("chain", "rows"), None),
        P(("chain", "rows"), None),
        P("chain", None, None, None),
    )
    out_specs = (P(("chain", "rows"), None), P(("chain", "rows"), None), P(("chain", "rows"), None))
    return jax.shard_map(
        on_device, mesh=mesh, in_specs=in_specs, out_specs=out_specs, check_vma=False
    )
```

```python
import jax
import numpy as np
import jax.numpy as jnp
from jax import lax
from jax.sharding import PartitionSpec as P

HALF_BAND = 256
LOAD_COLS = 256
LEVELS = 3


def spread_tips(top, bottom, row_pos, count, fanouts):
    stride = count
    for fanout in fanouts:
        step = stride // fanout
        got_top = top
        got_bottom = bottom
        for k in range(1, fanout):
            offset = k * step
            pairs = [(s, s + offset) for s in range(0, count, stride)]
            pairs += [(s, s - offset) for s in range(stride - 1, count, stride)]
            sent = jnp.where(row_pos % stride == 0, top, bottom)
            got = lax.ppermute(sent, "rows", pairs)
            got_top = jnp.where(row_pos % stride == offset, got, got_top)
            got_bottom = jnp.where(row_pos % stride == stride - 1 - offset, got, got_bottom)
        top = got_top
        bottom = got_bottom
        stride = step
    return top, bottom


def row_fanouts(count):
    fanouts = []
    while count > 1:
        fanout = 4 if count % 4 == 0 else 2
        fanouts.append(fanout)
        count //= fanout
    return fanouts


CORE_PLANS = (
    (((2, 0), (4, 0), (6, 0)), ((0, 1), (0, 2), (0, 3)), ((1, 0),)),
    (((0, 1), (0, 2), (0, 3)), ((2, 0), (4, 0), (6, 0)), ((7, 0),)),
)


def core_tree(top, bottom, chain_pos, row_pos, chain_count, z_count, y_count):
    row_count = z_count * y_count

    def moved(r, off, sign):
        z, y = divmod(r, y_count)
        return ((z + sign * off[0]) % z_count) * y_count + (y + sign * off[1]) % y_count

    holders = [({0}, {row_count - 1}) for _ in CORE_PLANS]
    for step in range(len(CORE_PLANS[0])):
        got_top = top
        got_bottom = bottom
        new_holders = [(set(t), set(b)) for t, b in holders]
        for slot in range(len(CORE_PLANS[0][step])):
            pairs = []
            sends_top = np.zeros((len(CORE_PLANS), row_count), bool)
            takes_top = np.zeros((len(CORE_PLANS), row_count), bool)
            takes_bottom = np.zeros((len(CORE_PLANS), row_count), bool)
            for kind, plan in enumerate(CORE_PLANS):
                off = plan[step][slot]
                tops, bottoms = holders[kind]
                for s in tops:
                    sends_top[kind, s] = True
                    d = moved(s, off, 1)
                    takes_top[kind, d] = True
                    new_holders[kind][0].add(d)
                for s in bottoms:
                    d = moved(s, off, -1)
                    takes_bottom[kind, d] = True
                    new_holders[kind][1].add(d)
                for c in range(kind, chain_count, len(CORE_PLANS)):
                    pairs += [(c * row_count + s, c * row_count + moved(s, off, 1)) for s in tops]
                    pairs += [(c * row_count + s, c * row_count + moved(s, off, -1)) for s in bottoms]
            kind_pos = chain_pos % len(CORE_PLANS)
            sent = jnp.where(jnp.asarray(sends_top)[kind_pos, row_pos], top, bottom)
            got = lax.ppermute(sent, ("chain", "rows"), pairs)
            got_top = jnp.where(jnp.asarray(takes_top)[kind_pos, row_pos], got, got_top)
            got_bottom = jnp.where(jnp.asarray(takes_bottom)[kind_pos, row_pos], got, got_bottom)
        holders = new_holders
        top = got_top
        bottom = got_bottom
    return top, bottom


def on_device(right_spike, left_spike, loads, tip_inverse):
    precise = lax.Precision.HIGH
    band = HALF_BAND
    width = LOAD_COLS
    chain_pos = lax.axis_index("chain")
    row_pos = lax.axis_index("rows")
    chain_count = lax.axis_size("chain")
    row_count = lax.axis_size("rows")
    spike_right = right_spike
    spike_left = left_spike
    load_block = loads
    inverses = [tip_inverse[0, 0]]
    for level in range(1, LEVELS):
        half = 2**level
        place = chain_pos % (2 * half)
        lasts = list(range(half - 1, chain_count - 1, 2 * half))
        mine = tip_inverse[0, level]
        for k in range(1, half):
            pairs = [(a, a - k) for a in lasts] + [(a + 1, a + 1 + k) for a in lasts]
            got = lax.ppermute(mine, "chain", pairs)
            mine = jnp.where((place == half - 1 - k) | (place == half + k), got, mine)
        inverses.append(mine)
    first_tip = jnp.concatenate([load_block[:band], spike_right[:band]], 1)
    last_tip = jnp.concatenate([load_block[-band:], spike_left[-band:]], 1)
    if row_count == 32 and chain_count % 2 == 0:
        top, bottom = core_tree(first_tip, last_tip, chain_pos, row_pos, chain_count, 8, 4)
    else:
        top, bottom = spread_tips(first_tip, last_tip, row_pos, row_count, row_fanouts(row_count))
    blank_block = jnp.zeros((band, band), jnp.float32)
    for level in range(LEVELS):
        half = 2**level
        place = chain_pos % (2 * half)
        side_low = place < half
        lasts = list(range(half - 1, chain_count - 1, 2 * half))
        lower_tip = bottom
        upper_tip = top
        sent = jnp.where(place == half - 1, bottom, top)
        for offset in list(range(-(half - 1), 0)) + list(range(1, half + 1)):
            pairs = [(a, a + offset) for a in lasts] + [(a + 1, a + 1 - offset) for a in lasts]
            got = lax.ppermute(sent, "chain", pairs)
            lower_tip = jnp.where(place == half - 1 + offset, got, lower_tip)
            upper_tip = jnp.where(place == half - offset, got, upper_tip)
        upper_rows = jnp.concatenate([lower_tip[:, :band], lower_tip[:, band:], blank_block], 1)
        lower_rows = jnp.concatenate([upper_tip[:, :band], blank_block, upper_tip[:, band:]], 1)
        tip_rhs = jnp.concatenate([upper_rows, lower_rows], 0)
        solved = jnp.dot(inverses[level], tip_rhs, precision=precise, preferred_element_type=jnp.float32)
        if level + 1 < LEVELS:
            bottom_prod = jnp.dot(
                bottom[:, band:], solved[:, : 2 * band], precision=precise, preferred_element_type=jnp.float32
            )
            bottom = jnp.concatenate([bottom[:, :band] - bottom_prod[:, :band], -bottom_prod[:, band:]], 1)
            top_prod = jnp.dot(
                top[:, band:],
                jnp.concatenate([solved[:, :band], solved[:, 2 * band :]], 1),
                precision=precise,
                preferred_element_type=jnp.float32,
            )
            top = jnp.concatenate([top[:, :band] - top_prod[:, :band], -top_prod[:, band:]], 1)
        driver = jnp.where(side_low, spike_right, spike_left)
        product = jnp.dot(driver, solved, precision=precise, preferred_element_type=jnp.float32)
        left_term = product[:, width : width + band]
        right_term = product[:, width + band :]
        load_block = load_block - product[:, :width]
        new_left = jnp.where(side_low, spike_left - left_term, -left_term)
        new_right = jnp.where(side_low, -right_term, spike_right - right_term)
        spike_left = new_left
        spike_right = new_right
    return (spike_right, spike_left, load_block)


def solution(mesh):
    in_specs = (
        P(("chain", "rows"), None),
        P(("chain", "rows"), None),
        P(("chain", "rows"), None),
        P("chain", None, None, None),
    )
    out_specs = (P(("chain", "rows"), None), P(("chain", "rows"), None), P(("chain", "rows"), None))
    return jax.shard_map(
        on_device, mesh=mesh, in_specs=in_specs, out_specs=out_specs, check_vma=False
    )
```

```python
import jax
import numpy as np
import jax.numpy as jnp
from jax import lax
from jax.sharding import PartitionSpec as P

HALF_BAND = 256
LOAD_COLS = 256
LEVELS = 3


def spread_tips(top, bottom, row_pos, count, fanouts):
    stride = count
    for fanout in fanouts:
        step = stride // fanout
        got_top = top
        got_bottom = bottom
        for k in range(1, fanout):
            offset = k * step
            pairs = [(s, s + offset) for s in range(0, count, stride)]
            pairs += [(s, s - offset) for s in range(stride - 1, count, stride)]
            sent = jnp.where(row_pos % stride == 0, top, bottom)
            got = lax.ppermute(sent, "rows", pairs)
            got_top = jnp.where(row_pos % stride == offset, got, got_top)
            got_bottom = jnp.where(row_pos % stride == stride - 1 - offset, got, got_bottom)
        top = got_top
        bottom = got_bottom
        stride = step
    return top, bottom


def row_fanouts(count):
    fanouts = []
    while count > 1:
        fanout = 4 if count % 4 == 0 else 2
        fanouts.append(fanout)
        count //= fanout
    return fanouts


CORE_PLANS = (
    (((2, 0), (4, 0), (6, 0)), ((0, 1), (0, 2), (0, 3)), ((1, 0),)),
    (((0, 1), (0, 2), (0, 3)), ((2, 0), (4, 0), (6, 0)), ((7, 0),)),
)


def core_tree(top, bottom, chain_pos, row_pos, chain_count, z_count, y_count):
    row_count = z_count * y_count
    kinds = len(CORE_PLANS)

    def moved(r, off, sign):
        z, y = divmod(r, y_count)
        return ((z + sign * off[0]) % z_count) * y_count + (y + sign * off[1]) % y_count

    steps = len(CORE_PLANS[0])
    table = np.zeros((steps, 3, kinds, row_count), np.int32)
    all_pairs = []
    holders = [({0}, {row_count - 1}) for _ in CORE_PLANS]
    for step in range(steps):
        new_holders = [(set(t), set(b)) for t, b in holders]
        step_pairs = []
        for slot in range(len(CORE_PLANS[0][step])):
            pairs = []
            for kind, plan in enumerate(CORE_PLANS):
                off = plan[step][slot]
                tops, bottoms = holders[kind]
                for s in tops:
                    table[step, 2, kind, s] = 1
                    d = moved(s, off, 1)
                    table[step, 0, kind, d] = slot + 1
                    new_holders[kind][0].add(d)
                for s in bottoms:
                    d = moved(s, off, -1)
                    table[step, 1, kind, d] = slot + 1
                    new_holders[kind][1].add(d)
                for c in range(kind, chain_count, kinds):
                    pairs += [(c * row_count + s, c * row_count + moved(s, off, 1)) for s in tops]
                    pairs += [(c * row_count + s, c * row_count + moved(s, off, -1)) for s in bottoms]
            step_pairs.append(pairs)
        all_pairs.append(step_pairs)
        holders = new_holders
    mine = jnp.asarray(table.reshape(steps * 3, kinds, row_count))[:, chain_pos % kinds, row_pos]
    for step in range(steps):
        sent = jnp.where(mine[3 * step + 2] == 1, top, bottom)
        got = [lax.ppermute(sent, ("chain", "rows"), pairs) for pairs in all_pairs[step]]
        top = lax.select_n(mine[3 * step], top, *got)
        bottom = lax.select_n(mine[3 * step + 1], bottom, *got)
    return top, bottom


def on_device(right_spike, left_spike, loads, tip_inverse):
    precise = lax.Precision.HIGHEST
    fast = lax.Precision.HIGH
    band = HALF_BAND
    width = LOAD_COLS
    chain_pos = lax.axis_index("chain")
    row_pos = lax.axis_index("rows")
    chain_count = lax.axis_size("chain")
    row_count = lax.axis_size("rows")
    spike_right = right_spike
    spike_left = left_spike
    load_block = loads
    inverses = [tip_inverse[0, 0]]
    for level in range(1, LEVELS):
        half = 2**level
        place = chain_pos % (2 * half)
        lasts = list(range(half - 1, chain_count - 1, 2 * half))
        mine = tip_inverse[0, level]
        for k in range(1, half):
            pairs = [(a, a - k) for a in lasts] + [(a + 1, a + 1 + k) for a in lasts]
            got = lax.ppermute(mine, "chain", pairs)
            mine = jnp.where((place == half - 1 - k) | (place == half + k), got, mine)
        inverses.append(mine)
    first_tip = jnp.concatenate([load_block[:band], spike_right[:band]], 1)
    last_tip = jnp.concatenate([load_block[-band:], spike_left[-band:]], 1)
    if row_count == 32 and chain_count % 2 == 0:
        top, bottom = core_tree(first_tip, last_tip, chain_pos, row_pos, chain_count, 8, 4)
    else:
        top, bottom = spread_tips(first_tip, last_tip, row_pos, row_count, row_fanouts(row_count))
    blank_block = jnp.zeros((band, band), jnp.float32)
    for level in range(LEVELS):
        half = 2**level
        place = chain_pos % (2 * half)
        side_low = place < half
        lasts = list(range(half - 1, chain_count - 1, 2 * half))
        lower_tip = bottom
        upper_tip = top
        sent = jnp.where(place == half - 1, bottom, top)
        for offset in list(range(-(half - 1), 0)) + list(range(1, half + 1)):
            pairs = [(a, a + offset) for a in lasts] + [(a + 1, a + 1 - offset) for a in lasts]
            got = lax.ppermute(sent, "chain", pairs)
            lower_tip = jnp.where(place == half - 1 + offset, got, lower_tip)
            upper_tip = jnp.where(place == half - offset, got, upper_tip)
        upper_rows = jnp.concatenate([lower_tip[:, :band], lower_tip[:, band:], blank_block], 1)
        lower_rows = jnp.concatenate([upper_tip[:, :band], blank_block, upper_tip[:, band:]], 1)
        tip_rhs = jnp.concatenate([upper_rows, lower_rows], 0)
        solved = jnp.dot(inverses[level], tip_rhs, precision=precise, preferred_element_type=jnp.float32)
        if level + 1 < LEVELS:
            bottom_prod = jnp.dot(
                bottom[:, band:], solved[:, : 2 * band], precision=precise, preferred_element_type=jnp.float32
            )
            bottom = jnp.concatenate([bottom[:, :band] - bottom_prod[:, :band], -bottom_prod[:, band:]], 1)
            top_prod = jnp.dot(
                top[:, band:],
                jnp.concatenate([solved[:, :band], solved[:, 2 * band :]], 1),
                precision=precise,
                preferred_element_type=jnp.float32,
            )
            top = jnp.concatenate([top[:, :band] - top_prod[:, :band], -top_prod[:, band:]], 1)
        driver = jnp.where(side_low, spike_right, spike_left)
        product = jnp.dot(driver, solved, precision=fast, preferred_element_type=jnp.float32)
        left_term = product[:, width : width + band]
        right_term = product[:, width + band :]
        load_block = load_block - product[:, :width]
        new_left = jnp.where(side_low, spike_left - left_term, -left_term)
        new_right = jnp.where(side_low, -right_term, spike_right - right_term)
        spike_left = new_left
        spike_right = new_right
    return (spike_right, spike_left, load_block)


def solution(mesh):
    in_specs = (
        P(("chain", "rows"), None),
        P(("chain", "rows"), None),
        P(("chain", "rows"), None),
        P("chain", None, None, None),
    )
    out_specs = (P(("chain", "rows"), None), P(("chain", "rows"), None), P(("chain", "rows"), None))
    return jax.shard_map(
        on_device, mesh=mesh, in_specs=in_specs, out_specs=out_specs, check_vma=False
    )
```

```python
import jax
import numpy as np
import jax.numpy as jnp
from jax import lax
from jax.experimental import pallas as pl
from jax.experimental.pallas import tpu as pltpu
from jax.sharding import PartitionSpec as P

HALF_BAND = 256
LOAD_COLS = 256
LEVELS = 3


def spread_tips(top, bottom, row_pos, count, fanouts):
    stride = count
    for fanout in fanouts:
        step = stride // fanout
        got_top = top
        got_bottom = bottom
        for k in range(1, fanout):
            offset = k * step
            pairs = [(s, s + offset) for s in range(0, count, stride)]
            pairs += [(s, s - offset) for s in range(stride - 1, count, stride)]
            sent = jnp.where(row_pos % stride == 0, top, bottom)
            got = lax.ppermute(sent, "rows", pairs)
            got_top = jnp.where(row_pos % stride == offset, got, got_top)
            got_bottom = jnp.where(row_pos % stride == stride - 1 - offset, got, got_bottom)
        top = got_top
        bottom = got_bottom
        stride = step
    return top, bottom


def row_fanouts(count):
    fanouts = []
    while count > 1:
        fanout = 4 if count % 4 == 0 else 2
        fanouts.append(fanout)
        count //= fanout
    return fanouts


def bulk_kernel(flag_ref, x_ref, v_ref, w_ref, g_ref, vo_ref, wo_ref, go_ref):
    low = flag_ref[0] == 1
    v = v_ref[...]
    w = w_ref[...]
    prod = jnp.dot(jnp.where(low, v, w), x_ref[...], precision=lax.Precision.HIGHEST,
                   preferred_element_type=jnp.float32)
    go_ref[...] = g_ref[...] - prod[:, :LOAD_COLS]
    left_term = prod[:, LOAD_COLS:LOAD_COLS + HALF_BAND]
    right_term = prod[:, LOAD_COLS + HALF_BAND:]
    wo_ref[...] = jnp.where(low, w - left_term, -left_term)
    vo_ref[...] = jnp.where(low, -right_term, v - right_term)

def bulk_update(flag, x, v, w, g, tile=512):
    rows = v.shape[0]
    block = pl.BlockSpec((tile, HALF_BAND), lambda i, f: (i, 0))
    out = jax.ShapeDtypeStruct((rows, HALF_BAND), jnp.float32)
    return pl.pallas_call(
        bulk_kernel,
        grid_spec=pltpu.PrefetchScalarGridSpec(
            num_scalar_prefetch=1,
            grid=(rows // tile,),
            in_specs=[pl.BlockSpec(x.shape, lambda i, f: (0, 0)), block, block, block],
            out_specs=[block, block, block],
        ),
        out_shape=[out, out, out],
    )(flag, x, v, w, g)


CORE_PLANS = (
    (((2, 0), (4, 0), (6, 0)), ((0, 1), (0, 2), (0, 3)), ((1, 0),)),
    (((0, 1), (0, 2), (0, 3)), ((2, 0), (4, 0), (6, 0)), ((7, 0),)),
)


def core_tree(top, bottom, chain_pos, row_pos, chain_count, z_count, y_count):
    row_count = z_count * y_count
    kinds = len(CORE_PLANS)

    def moved(r, off, sign):
        z, y = divmod(r, y_count)
        return ((z + sign * off[0]) % z_count) * y_count + (y + sign * off[1]) % y_count

    steps = len(CORE_PLANS[0])
    table = np.zeros((steps, 3, kinds, row_count), np.int32)
    all_pairs = []
    holders = [({0}, {row_count - 1}) for _ in CORE_PLANS]
    for step in range(steps):
        new_holders = [(set(t), set(b)) for t, b in holders]
        step_pairs = []
        for slot in range(len(CORE_PLANS[0][step])):
            pairs = []
            for kind, plan in enumerate(CORE_PLANS):
                off = plan[step][slot]
                tops, bottoms = holders[kind]
                for s in tops:
                    table[step, 2, kind, s] = 1
                    d = moved(s, off, 1)
                    table[step, 0, kind, d] = slot + 1
                    new_holders[kind][0].add(d)
                for s in bottoms:
                    d = moved(s, off, -1)
                    table[step, 1, kind, d] = slot + 1
                    new_holders[kind][1].add(d)
                for c in range(kind, chain_count, kinds):
                    pairs += [(c * row_count + s, c * row_count + moved(s, off, 1)) for s in tops]
                    pairs += [(c * row_count + s, c * row_count + moved(s, off, -1)) for s in bottoms]
            step_pairs.append(pairs)
        all_pairs.append(step_pairs)
        holders = new_holders
    mine = jnp.asarray(table.reshape(steps * 3, kinds, row_count))[:, chain_pos % kinds, row_pos]
    for step in range(steps):
        sent = jnp.where(mine[3 * step + 2] == 1, top, bottom)
        got = [lax.ppermute(sent, ("chain", "rows"), pairs) for pairs in all_pairs[step]]
        top = lax.select_n(mine[3 * step], top, *got)
        bottom = lax.select_n(mine[3 * step + 1], bottom, *got)
    return top, bottom


def on_device(right_spike, left_spike, loads, tip_inverse):
    precise = lax.Precision.HIGHEST
    band = HALF_BAND
    width = LOAD_COLS
    chain_pos = lax.axis_index("chain")
    row_pos = lax.axis_index("rows")
    chain_count = lax.axis_size("chain")
    row_count = lax.axis_size("rows")
    spike_right = right_spike
    spike_left = left_spike
    load_block = loads
    inverses = [tip_inverse[0, 0]]
    for level in range(1, LEVELS):
        half = 2**level
        place = chain_pos % (2 * half)
        lasts = list(range(half - 1, chain_count - 1, 2 * half))
        mine = tip_inverse[0, level]
        for k in range(1, half):
            pairs = [(a, a - k) for a in lasts] + [(a + 1, a + 1 + k) for a in lasts]
            got = lax.ppermute(mine, "chain", pairs)
            mine = jnp.where((place == half - 1 - k) | (place == half + k), got, mine)
        inverses.append(mine)
    first_tip = jnp.concatenate([load_block[:band], spike_right[:band]], 1)
    last_tip = jnp.concatenate([load_block[-band:], spike_left[-band:]], 1)
    if row_count == 32 and chain_count % 2 == 0:
        top, bottom = core_tree(first_tip, last_tip, chain_pos, row_pos, chain_count, 8, 4)
    else:
        top, bottom = spread_tips(first_tip, last_tip, row_pos, row_count, row_fanouts(row_count))
    blank_block = jnp.zeros((band, band), jnp.float32)
    for level in range(LEVELS):
        half = 2**level
        place = chain_pos % (2 * half)
        side_low = place < half
        lasts = list(range(half - 1, chain_count - 1, 2 * half))
        lower_tip = bottom
        upper_tip = top
        sent = jnp.where(place == half - 1, bottom, top)
        for offset in list(range(-(half - 1), 0)) + list(range(1, half + 1)):
            pairs = [(a, a + offset) for a in lasts] + [(a + 1, a + 1 - offset) for a in lasts]
            got = lax.ppermute(sent, "chain", pairs)
            lower_tip = jnp.where(place == half - 1 + offset, got, lower_tip)
            upper_tip = jnp.where(place == half - offset, got, upper_tip)
        upper_rows = jnp.concatenate([lower_tip[:, :band], lower_tip[:, band:], blank_block], 1)
        lower_rows = jnp.concatenate([upper_tip[:, :band], blank_block, upper_tip[:, band:]], 1)
        tip_rhs = jnp.concatenate([upper_rows, lower_rows], 0)
        solved = jnp.dot(inverses[level], tip_rhs, precision=precise, preferred_element_type=jnp.float32)
        if level + 1 < LEVELS:
            bottom_prod = jnp.dot(
                bottom[:, band:], solved[:, : 2 * band], precision=precise, preferred_element_type=jnp.float32
            )
            bottom = jnp.concatenate([bottom[:, :band] - bottom_prod[:, :band], -bottom_prod[:, band:]], 1)
            top_prod = jnp.dot(
                top[:, band:],
                jnp.concatenate([solved[:, :band], solved[:, 2 * band :]], 1),
                precision=precise,
                preferred_element_type=jnp.float32,
            )
            top = jnp.concatenate([top[:, :band] - top_prod[:, :band], -top_prod[:, band:]], 1)
        flag = jnp.where(side_low, 1, 0).astype(jnp.int32).reshape(1)
        spike_right, spike_left, load_block = bulk_update(flag, solved, spike_right, spike_left, load_block)
    return (spike_right, spike_left, load_block)


def solution(mesh):
    in_specs = (
        P(("chain", "rows"), None),
        P(("chain", "rows"), None),
        P(("chain", "rows"), None),
        P("chain", None, None, None),
    )
    out_specs = (P(("chain", "rows"), None), P(("chain", "rows"), None), P(("chain", "rows"), None))
    return jax.shard_map(
        on_device, mesh=mesh, in_specs=in_specs, out_specs=out_specs, check_vma=False
    )
```

```python
import jax
import numpy as np
import jax.numpy as jnp
from jax import lax
from jax.experimental import pallas as pl
from jax.experimental.pallas import tpu as pltpu
from jax.sharding import PartitionSpec as P

HALF_BAND = 256
LOAD_COLS = 256
LEVELS = 3


def spread_tips(top, bottom, row_pos, count, fanouts):
    stride = count
    for fanout in fanouts:
        step = stride // fanout
        got_top = top
        got_bottom = bottom
        for k in range(1, fanout):
            offset = k * step
            pairs = [(s, s + offset) for s in range(0, count, stride)]
            pairs += [(s, s - offset) for s in range(stride - 1, count, stride)]
            sent = jnp.where(row_pos % stride == 0, top, bottom)
            got = lax.ppermute(sent, "rows", pairs)
            got_top = jnp.where(row_pos % stride == offset, got, got_top)
            got_bottom = jnp.where(row_pos % stride == stride - 1 - offset, got, got_bottom)
        top = got_top
        bottom = got_bottom
        stride = step
    return top, bottom


def row_fanouts(count):
    fanouts = []
    while count > 1:
        fanout = 4 if count % 4 == 0 else 2
        fanouts.append(fanout)
        count //= fanout
    return fanouts


def bulk_kernel(flag_ref, x_ref, v_ref, w_ref, g_ref, vo_ref, wo_ref, go_ref):
    low = flag_ref[0] == 1
    v = v_ref[...]
    w = w_ref[...]
    driver = jnp.where(low, v, w)
    d_hi = driver.astype(jnp.bfloat16)
    d_lo = (driver - d_hi.astype(jnp.float32)).astype(jnp.bfloat16)
    x = x_ref[...]
    x_hi = x.astype(jnp.bfloat16)
    x_lo = (x - x_hi.astype(jnp.float32)).astype(jnp.bfloat16)
    prod = jnp.dot(d_hi, x_hi, preferred_element_type=jnp.float32)
    prod += jnp.dot(d_hi, x_lo, preferred_element_type=jnp.float32)
    prod += jnp.dot(d_lo, x_hi, preferred_element_type=jnp.float32)
    go_ref[...] = g_ref[...] - prod[:, :LOAD_COLS]
    left_term = prod[:, LOAD_COLS:LOAD_COLS + HALF_BAND]
    right_term = prod[:, LOAD_COLS + HALF_BAND:]
    wo_ref[...] = jnp.where(low, w - left_term, -left_term)
    vo_ref[...] = jnp.where(low, -right_term, v - right_term)


def bulk_update(flag, x, v, w, g, tile=512):
    rows = v.shape[0]
    block = pl.BlockSpec((tile, HALF_BAND), lambda i, f: (i, 0))
    out = jax.ShapeDtypeStruct((rows, HALF_BAND), jnp.float32)
    return pl.pallas_call(
        bulk_kernel,
        grid_spec=pltpu.PrefetchScalarGridSpec(
            num_scalar_prefetch=1,
            grid=(rows // tile,),
            in_specs=[pl.BlockSpec(x.shape, lambda i, f: (0, 0)), block, block, block],
            out_specs=[block, block, block],
        ),
        out_shape=[out, out, out],
    )(flag, x, v, w, g)


CORE_PLANS = (
    (((2, 0), (4, 0), (6, 0)), ((0, 1), (0, 2), (0, 3)), ((1, 0),)),
    (((0, 1), (0, 2), (0, 3)), ((2, 0), (4, 0), (6, 0)), ((7, 0),)),
)


def core_tree(top, bottom, chain_pos, row_pos, chain_count, z_count, y_count):
    row_count = z_count * y_count
    kinds = len(CORE_PLANS)

    def moved(r, off, sign):
        z, y = divmod(r, y_count)
        return ((z + sign * off[0]) % z_count) * y_count + (y + sign * off[1]) % y_count

    steps = len(CORE_PLANS[0])
    table = np.zeros((steps, 3, kinds, row_count), np.int32)
    all_pairs = []
    holders = [({0}, {row_count - 1}) for _ in CORE_PLANS]
    for step in range(steps):
        new_holders = [(set(t), set(b)) for t, b in holders]
        step_pairs = []
        for slot in range(len(CORE_PLANS[0][step])):
            pairs = []
            for kind, plan in enumerate(CORE_PLANS):
                off = plan[step][slot]
                tops, bottoms = holders[kind]
                for s in tops:
                    table[step, 2, kind, s] = 1
                    d = moved(s, off, 1)
                    table[step, 0, kind, d] = slot + 1
                    new_holders[kind][0].add(d)
                for s in bottoms:
                    d = moved(s, off, -1)
                    table[step, 1, kind, d] = slot + 1
                    new_holders[kind][1].add(d)
                for c in range(kind, chain_count, kinds):
                    pairs += [(c * row_count + s, c * row_count + moved(s, off, 1)) for s in tops]
                    pairs += [(c * row_count + s, c * row_count + moved(s, off, -1)) for s in bottoms]
            step_pairs.append(pairs)
        all_pairs.append(step_pairs)
        holders = new_holders
    mine = jnp.asarray(table.reshape(steps * 3, kinds, row_count))[:, chain_pos % kinds, row_pos]
    for step in range(steps):
        sent = jnp.where(mine[3 * step + 2] == 1, top, bottom)
        got = [lax.ppermute(sent, ("chain", "rows"), pairs) for pairs in all_pairs[step]]
        top = lax.select_n(mine[3 * step], top, *got)
        bottom = lax.select_n(mine[3 * step + 1], bottom, *got)
    return top, bottom


def on_device(right_spike, left_spike, loads, tip_inverse):
    precise = lax.Precision.HIGHEST
    band = HALF_BAND
    width = LOAD_COLS
    chain_pos = lax.axis_index("chain")
    row_pos = lax.axis_index("rows")
    chain_count = lax.axis_size("chain")
    row_count = lax.axis_size("rows")
    spike_right = right_spike
    spike_left = left_spike
    load_block = loads
    inverses = [tip_inverse[0, 0]]
    for level in range(1, LEVELS):
        half = 2**level
        place = chain_pos % (2 * half)
        lasts = list(range(half - 1, chain_count - 1, 2 * half))
        mine = tip_inverse[0, level]
        for k in range(1, half):
            pairs = [(a, a - k) for a in lasts] + [(a + 1, a + 1 + k) for a in lasts]
            got = lax.ppermute(mine, "chain", pairs)
            mine = jnp.where((place == half - 1 - k) | (place == half + k), got, mine)
        inverses.append(mine)
    first_tip = jnp.concatenate([load_block[:band], spike_right[:band]], 1)
    last_tip = jnp.concatenate([load_block[-band:], spike_left[-band:]], 1)
    if row_count == 32 and chain_count % 2 == 0:
        top, bottom = core_tree(first_tip, last_tip, chain_pos, row_pos, chain_count, 8, 4)
    else:
        top, bottom = spread_tips(first_tip, last_tip, row_pos, row_count, row_fanouts(row_count))
    inverses, top, bottom = lax.optimization_barrier((inverses, top, bottom))
    blank_block = jnp.zeros((band, band), jnp.float32)
    for level in range(LEVELS):
        half = 2**level
        place = chain_pos % (2 * half)
        side_low = place < half
        lasts = list(range(half - 1, chain_count - 1, 2 * half))
        lower_tip = bottom
        upper_tip = top
        sent = jnp.where(place == half - 1, bottom, top)
        for offset in list(range(-(half - 1), 0)) + list(range(1, half + 1)):
            pairs = [(a, a + offset) for a in lasts] + [(a + 1, a + 1 - offset) for a in lasts]
            got = lax.ppermute(sent, "chain", pairs)
            lower_tip = jnp.where(place == half - 1 + offset, got, lower_tip)
            upper_tip = jnp.where(place == half - offset, got, upper_tip)
        upper_rows = jnp.concatenate([lower_tip[:, :band], lower_tip[:, band:], blank_block], 1)
        lower_rows = jnp.concatenate([upper_tip[:, :band], blank_block, upper_tip[:, band:]], 1)
        tip_rhs = jnp.concatenate([upper_rows, lower_rows], 0)
        solved = jnp.dot(inverses[level], tip_rhs, precision=precise, preferred_element_type=jnp.float32)
        if level + 1 < LEVELS:
            bottom_prod = jnp.dot(
                bottom[:, band:], solved[:, : 2 * band], precision=precise, preferred_element_type=jnp.float32
            )
            bottom = jnp.concatenate([bottom[:, :band] - bottom_prod[:, :band], -bottom_prod[:, band:]], 1)
            top_prod = jnp.dot(
                top[:, band:],
                jnp.concatenate([solved[:, :band], solved[:, 2 * band :]], 1),
                precision=precise,
                preferred_element_type=jnp.float32,
            )
            top = jnp.concatenate([top[:, :band] - top_prod[:, :band], -top_prod[:, band:]], 1)
        flag = jnp.where(side_low, 1, 0).astype(jnp.int32).reshape(1)
        spike_right, spike_left, load_block = bulk_update(flag, solved, spike_right, spike_left, load_block)
    return (spike_right, spike_left, load_block)


def solution(mesh):
    in_specs = (
        P(("chain", "rows"), None),
        P(("chain", "rows"), None),
        P(("chain", "rows"), None),
        P("chain", None, None, None),
    )
    out_specs = (P(("chain", "rows"), None), P(("chain", "rows"), None), P(("chain", "rows"), None))
    return jax.shard_map(
        on_device, mesh=mesh, in_specs=in_specs, out_specs=out_specs, check_vma=False
    )
```

```python
import jax
import numpy as np
import jax.numpy as jnp
from jax import lax
from jax.experimental import pallas as pl
from jax.experimental.pallas import tpu as pltpu
from jax.sharding import PartitionSpec as P

HALF_BAND = 256
LOAD_COLS = 256
LEVELS = 3


def spread_tips(top, bottom, row_pos, count, fanouts):
    stride = count
    for fanout in fanouts:
        step = stride // fanout
        got_top = top
        got_bottom = bottom
        for k in range(1, fanout):
            offset = k * step
            pairs = [(s, s + offset) for s in range(0, count, stride)]
            pairs += [(s, s - offset) for s in range(stride - 1, count, stride)]
            sent = jnp.where(row_pos % stride == 0, top, bottom)
            got = lax.ppermute(sent, "rows", pairs)
            got_top = jnp.where(row_pos % stride == offset, got, got_top)
            got_bottom = jnp.where(row_pos % stride == stride - 1 - offset, got, got_bottom)
        top = got_top
        bottom = got_bottom
        stride = step
    return top, bottom


def row_fanouts(count):
    fanouts = []
    while count > 1:
        fanout = 4 if count % 4 == 0 else 2
        fanouts.append(fanout)
        count //= fanout
    return fanouts


def bulk_kernel(flag_ref, x_ref, v_ref, w_ref, g_ref, vo_ref, wo_ref, go_ref):
    low = flag_ref[0] == 1
    v = v_ref[...]
    w = w_ref[...]
    driver = jnp.where(low, v, w)
    d_hi = driver.astype(jnp.bfloat16)
    d_lo = (driver - d_hi.astype(jnp.float32)).astype(jnp.bfloat16)
    x = x_ref[...]
    x_hi = x.astype(jnp.bfloat16)
    x_lo = (x - x_hi.astype(jnp.float32)).astype(jnp.bfloat16)
    prod = jnp.dot(d_hi, x_hi, preferred_element_type=jnp.float32)
    prod += jnp.dot(d_hi, x_lo, preferred_element_type=jnp.float32)
    prod += jnp.dot(d_lo, x_hi, preferred_element_type=jnp.float32)
    go_ref[...] = g_ref[...] - prod[:, :LOAD_COLS]
    left_term = prod[:, LOAD_COLS:LOAD_COLS + HALF_BAND]
    right_term = prod[:, LOAD_COLS + HALF_BAND:]
    wo_ref[...] = jnp.where(low, w - left_term, -left_term)
    vo_ref[...] = jnp.where(low, -right_term, v - right_term)


def bulk_update(flag, x, v, w, g, tile=512):
    rows = v.shape[0]
    block = pl.BlockSpec((tile, HALF_BAND), lambda i, f: (i, 0))
    out = jax.ShapeDtypeStruct((rows, HALF_BAND), jnp.float32)
    return pl.pallas_call(
        bulk_kernel,
        grid_spec=pltpu.PrefetchScalarGridSpec(
            num_scalar_prefetch=1,
            grid=(rows // tile,),
            in_specs=[pl.BlockSpec(x.shape, lambda i, f: (0, 0)), block, block, block],
            out_specs=[block, block, block],
        ),
        out_shape=[out, out, out],
    )(flag, x, v, w, g)


CORE_PLANS = (
    (((2, 0), (4, 0), (6, 0)), ((0, 1), (0, 2), (0, 3)), ((1, 0),)),
    (((0, 1), (0, 2), (0, 3)), ((2, 0), (4, 0), (6, 0)), ((7, 0),)),
)


def core_tree(top, bottom, chain_pos, row_pos, chain_count, z_count, y_count):
    row_count = z_count * y_count
    kinds = len(CORE_PLANS)

    def moved(r, off, sign):
        z, y = divmod(r, y_count)
        return ((z + sign * off[0]) % z_count) * y_count + (y + sign * off[1]) % y_count

    steps = len(CORE_PLANS[0])
    table = np.zeros((steps, 3, kinds, row_count), np.int32)
    all_pairs = []
    holders = [({0}, {row_count - 1}) for _ in CORE_PLANS]
    for step in range(steps):
        new_holders = [(set(t), set(b)) for t, b in holders]
        step_pairs = []
        for slot in range(len(CORE_PLANS[0][step])):
            pairs = []
            for kind, plan in enumerate(CORE_PLANS):
                off = plan[step][slot]
                tops, bottoms = holders[kind]
                for s in tops:
                    table[step, 2, kind, s] = 1
                    d = moved(s, off, 1)
                    table[step, 0, kind, d] = slot + 1
                    new_holders[kind][0].add(d)
                for s in bottoms:
                    d = moved(s, off, -1)
                    table[step, 1, kind, d] = slot + 1
                    new_holders[kind][1].add(d)
                for c in range(kind, chain_count, kinds):
                    pairs += [(c * row_count + s, c * row_count + moved(s, off, 1)) for s in tops]
                    pairs += [(c * row_count + s, c * row_count + moved(s, off, -1)) for s in bottoms]
            step_pairs.append(pairs)
        all_pairs.append(step_pairs)
        holders = new_holders
    mine = jnp.asarray(table.reshape(steps * 3, kinds, row_count))[:, chain_pos % kinds, row_pos]
    for step in range(steps):
        sent = jnp.where(mine[3 * step + 2] == 1, top, bottom)
        got = [lax.ppermute(sent, ("chain", "rows"), pairs) for pairs in all_pairs[step]]
        top = lax.select_n(mine[3 * step], top, *got)
        bottom = lax.select_n(mine[3 * step + 1], bottom, *got)
    return top, bottom


def on_device(right_spike, left_spike, loads, tip_inverse):
    precise = lax.Precision.HIGHEST
    band = HALF_BAND
    width = LOAD_COLS
    chain_pos = lax.axis_index("chain")
    row_pos = lax.axis_index("rows")
    chain_count = lax.axis_size("chain")
    row_count = lax.axis_size("rows")
    spike_right = right_spike
    spike_left = left_spike
    load_block = loads
    inverses = [tip_inverse[0, 0]]
    for level in range(1, LEVELS):
        half = 2**level
        place = chain_pos % (2 * half)
        lasts = list(range(half - 1, chain_count - 1, 2 * half))
        mine = tip_inverse[0, level]
        for k in range(1, half):
            pairs = [(a, a - k) for a in lasts] + [(a + 1, a + 1 + k) for a in lasts]
            got = lax.ppermute(mine, "chain", pairs)
            mine = jnp.where((place == half - 1 - k) | (place == half + k), got, mine)
        inverses.append(mine)
    first_tip = jnp.concatenate([load_block[:band], spike_right[:band]], 1)
    last_tip = jnp.concatenate([load_block[-band:], spike_left[-band:]], 1)
    if row_count == 32 and chain_count % 2 == 0:
        top, bottom = core_tree(first_tip, last_tip, chain_pos, row_pos, chain_count, 8, 4)
    else:
        top, bottom = spread_tips(first_tip, last_tip, row_pos, row_count, row_fanouts(row_count))
    inverses, top, bottom = lax.optimization_barrier((inverses, top, bottom))
    blank_block = jnp.zeros((band, band), jnp.float32)
    for level in range(LEVELS):
        half = 2**level
        place = chain_pos % (2 * half)
        side_low = place < half
        lasts = list(range(half - 1, chain_count - 1, 2 * half))
        lower_tip = bottom
        upper_tip = top
        sent = jnp.where(place == half - 1, bottom, top)
        for offset in list(range(-(half - 1), 0)) + list(range(1, half + 1)):
            pairs = [(a, a + offset) for a in lasts] + [(a + 1, a + 1 - offset) for a in lasts]
            got = lax.ppermute(sent, "chain", pairs)
            lower_tip = jnp.where(place == half - 1 + offset, got, lower_tip)
            upper_tip = jnp.where(place == half - offset, got, upper_tip)
        if level > 0:
            lower_tip, upper_tip, spike_right, spike_left, load_block = lax.optimization_barrier(
                (lower_tip, upper_tip, spike_right, spike_left, load_block)
            )
        upper_rows = jnp.concatenate([lower_tip[:, :band], lower_tip[:, band:], blank_block], 1)
        lower_rows = jnp.concatenate([upper_tip[:, :band], blank_block, upper_tip[:, band:]], 1)
        tip_rhs = jnp.concatenate([upper_rows, lower_rows], 0)
        solved = jnp.dot(inverses[level], tip_rhs, precision=precise, preferred_element_type=jnp.float32)
        if level + 1 < LEVELS:
            bottom_prod = jnp.dot(
                bottom[:, band:], solved[:, : 2 * band], precision=precise, preferred_element_type=jnp.float32
            )
            bottom = jnp.concatenate([bottom[:, :band] - bottom_prod[:, :band], -bottom_prod[:, band:]], 1)
            top_prod = jnp.dot(
                top[:, band:],
                jnp.concatenate([solved[:, :band], solved[:, 2 * band :]], 1),
                precision=precise,
                preferred_element_type=jnp.float32,
            )
            top = jnp.concatenate([top[:, :band] - top_prod[:, :band], -top_prod[:, band:]], 1)
        flag = jnp.where(side_low, 1, 0).astype(jnp.int32).reshape(1)
        spike_right, spike_left, load_block = bulk_update(flag, solved, spike_right, spike_left, load_block)
    return (spike_right, spike_left, load_block)


def solution(mesh):
    in_specs = (
        P(("chain", "rows"), None),
        P(("chain", "rows"), None),
        P(("chain", "rows"), None),
        P("chain", None, None, None),
    )
    out_specs = (P(("chain", "rows"), None), P(("chain", "rows"), None), P(("chain", "rows"), None))
    return jax.shard_map(
        on_device, mesh=mesh, in_specs=in_specs, out_specs=out_specs, check_vma=False
    )
```

```python
import jax
import numpy as np
import jax.numpy as jnp
from jax import lax
from jax.experimental import pallas as pl
from jax.experimental.pallas import tpu as pltpu
from jax.sharding import PartitionSpec as P


HALF_BAND = 256
LOAD_COLS = 256
LEVELS = 3


def spread_tips(top, bottom, row_pos, count, fanouts):
    stride = count
    for fanout in fanouts:
        step = stride // fanout
        got_top = top
        got_bottom = bottom
        for k in range(1, fanout):
            offset = k * step
            pairs = [(s, s + offset) for s in range(0, count, stride)]
            pairs += [(s, s - offset) for s in range(stride - 1, count, stride)]
            sent = jnp.where(row_pos % stride == 0, top, bottom)
            got = lax.ppermute(sent, "rows", pairs)
            got_top = jnp.where(row_pos % stride == offset, got, got_top)
            got_bottom = jnp.where(row_pos % stride == stride - 1 - offset, got, got_bottom)
        top = got_top
        bottom = got_bottom
        stride = step
    return top, bottom


def row_fanouts(count):
    fanouts = []
    while count > 1:
        fanout = 4 if count % 4 == 0 else 2
        fanouts.append(fanout)
        count //= fanout
    return fanouts


def bulk_kernel(flag_ref, x_ref, v_ref, w_ref, g_ref, vo_ref, wo_ref, go_ref):
    low = flag_ref[0] == 1
    v = v_ref[...]
    w = w_ref[...]
    driver = jnp.where(low, v, w)
    d_hi = driver.astype(jnp.bfloat16)
    d_lo = (driver - d_hi.astype(jnp.float32)).astype(jnp.bfloat16)
    x = x_ref[...]
    x_hi = x.astype(jnp.bfloat16)
    x_lo = (x - x_hi.astype(jnp.float32)).astype(jnp.bfloat16)
    prod = jnp.dot(d_hi, x_hi, preferred_element_type=jnp.float32)
    prod += jnp.dot(d_hi, x_lo, preferred_element_type=jnp.float32)
    prod += jnp.dot(d_lo, x_hi, preferred_element_type=jnp.float32)
    go_ref[...] = g_ref[...] - prod[:, :LOAD_COLS]
    left_term = prod[:, LOAD_COLS:LOAD_COLS + HALF_BAND]
    right_term = prod[:, LOAD_COLS + HALF_BAND:]
    wo_ref[...] = jnp.where(low, w - left_term, -left_term)
    vo_ref[...] = jnp.where(low, -right_term, v - right_term)


def bulk_update(flag, x, v, w, g, tile=256):
    rows = v.shape[0]
    block = pl.BlockSpec((tile, HALF_BAND), lambda i, f: (i, 0))
    out = jax.ShapeDtypeStruct((rows, HALF_BAND), jnp.float32)
    return pl.pallas_call(
        bulk_kernel,
        grid_spec=pltpu.PrefetchScalarGridSpec(
            num_scalar_prefetch=1,
            grid=(rows // tile,),
            in_specs=[pl.BlockSpec(x.shape, lambda i, f: (0, 0)), block, block, block],
            out_specs=[block, block, block],
        ),
        out_shape=[out, out, out],
    )(flag, x, v, w, g)


CORE_PLANS = (
    (((2, 0), (4, 0), (6, 0)), ((0, 1), (0, 2), (0, 3)), ((1, 0),)),
    (((0, 1), (0, 2), (0, 3)), ((2, 0), (4, 0), (6, 0)), ((7, 0),)),
)


def core_tree(top, bottom, chain_pos, row_pos, chain_count, z_count, y_count):
    row_count = z_count * y_count
    kinds = len(CORE_PLANS)

    def moved(r, off, sign):
        z, y = divmod(r, y_count)
        return ((z + sign * off[0]) % z_count) * y_count + (y + sign * off[1]) % y_count

    steps = len(CORE_PLANS[0])
    table = np.zeros((steps, 3, kinds, row_count), np.int32)
    all_pairs = []
    holders = [({0}, {row_count - 1}) for _ in CORE_PLANS]
    for step in range(steps):
        new_holders = [(set(t), set(b)) for t, b in holders]
        step_pairs = []
        for slot in range(len(CORE_PLANS[0][step])):
            pairs = []
            for kind, plan in enumerate(CORE_PLANS):
                off = plan[step][slot]
                tops, bottoms = holders[kind]
                for s in tops:
                    table[step, 2, kind, s] = 1
                    d = moved(s, off, 1)
                    table[step, 0, kind, d] = slot + 1
                    new_holders[kind][0].add(d)
                for s in bottoms:
                    d = moved(s, off, -1)
                    table[step, 1, kind, d] = slot + 1
                    new_holders[kind][1].add(d)
                for c in range(kind, chain_count, kinds):
                    pairs += [(c * row_count + s, c * row_count + moved(s, off, 1)) for s in tops]
                    pairs += [(c * row_count + s, c * row_count + moved(s, off, -1)) for s in bottoms]
            step_pairs.append(pairs)
        all_pairs.append(step_pairs)
        holders = new_holders
    mine = jnp.asarray(table.reshape(steps * 3, kinds, row_count))[:, chain_pos % kinds, row_pos]
    for step in range(steps):
        sent = jnp.where(mine[3 * step + 2] == 1, top, bottom)
        got = [lax.ppermute(sent, ("chain", "rows"), pairs) for pairs in all_pairs[step]]
        top = lax.select_n(mine[3 * step], top, *got)
        bottom = lax.select_n(mine[3 * step + 1], bottom, *got)
    return top, bottom


def on_device(right_spike, left_spike, loads, tip_inverse):
    precise = lax.Precision.HIGHEST
    band = HALF_BAND
    width = LOAD_COLS
    chain_pos = lax.axis_index("chain")
    row_pos = lax.axis_index("rows")
    chain_count = lax.axis_size("chain")
    row_count = lax.axis_size("rows")
    spike_right = right_spike
    spike_left = left_spike
    load_block = loads
    inverses = [tip_inverse[0, 0]]
    for level in range(1, LEVELS):
        half = 2**level
        place = chain_pos % (2 * half)
        lasts = list(range(half - 1, chain_count - 1, 2 * half))
        mine = tip_inverse[0, level]
        for k in range(1, half):
            pairs = [(a, a - k) for a in lasts] + [(a + 1, a + 1 + k) for a in lasts]
            got = lax.ppermute(mine, "chain", pairs)
            mine = jnp.where((place == half - 1 - k) | (place == half + k), got, mine)
        inverses.append(mine)
    first_tip = jnp.concatenate([load_block[:band], spike_right[:band]], 1)
    last_tip = jnp.concatenate([load_block[-band:], spike_left[-band:]], 1)
    if row_count == 32 and chain_count % 2 == 0:
        top, bottom = core_tree(first_tip, last_tip, chain_pos, row_pos, chain_count, 8, 4)
    else:
        top, bottom = spread_tips(first_tip, last_tip, row_pos, row_count, row_fanouts(row_count))
    inverses, top, bottom = lax.optimization_barrier((inverses, top, bottom))
    blank_block = jnp.zeros((band, band), jnp.float32)
    for level in range(LEVELS):
        half = 2**level
        place = chain_pos % (2 * half)
        side_low = place < half
        lasts = list(range(half - 1, chain_count - 1, 2 * half))
        lower_tip = bottom
        upper_tip = top
        sent = jnp.where(place == half - 1, bottom, top)
        for offset in list(range(-(half - 1), 0)) + list(range(1, half + 1)):
            pairs = [(a, a + offset) for a in lasts] + [(a + 1, a + 1 - offset) for a in lasts]
            got = lax.ppermute(sent, "chain", pairs)
            lower_tip = jnp.where(place == half - 1 + offset, got, lower_tip)
            upper_tip = jnp.where(place == half - offset, got, upper_tip)
        if level > 0:
            lower_tip, upper_tip, spike_right, spike_left, load_block = lax.optimization_barrier(
                (lower_tip, upper_tip, spike_right, spike_left, load_block)
            )
        upper_rows = jnp.concatenate([lower_tip[:, :band], lower_tip[:, band:], blank_block], 1)
        lower_rows = jnp.concatenate([upper_tip[:, :band], blank_block, upper_tip[:, band:]], 1)
        tip_rhs = jnp.concatenate([upper_rows, lower_rows], 0)
        solved = jnp.dot(inverses[level], tip_rhs, precision=precise, preferred_element_type=jnp.float32)
        if level + 1 < LEVELS:
            bottom_prod = jnp.dot(
                bottom[:, band:], solved[:, : 2 * band], precision=precise, preferred_element_type=jnp.float32
            )
            bottom = jnp.concatenate([bottom[:, :band] - bottom_prod[:, :band], -bottom_prod[:, band:]], 1)
            top_prod = jnp.dot(
                top[:, band:],
                jnp.concatenate([solved[:, :band], solved[:, 2 * band :]], 1),
                precision=precise,
                preferred_element_type=jnp.float32,
            )
            top = jnp.concatenate([top[:, :band] - top_prod[:, :band], -top_prod[:, band:]], 1)
        flag = jnp.where(side_low, 1, 0).astype(jnp.int32).reshape(1)
        spike_right, spike_left, load_block = bulk_update(flag, solved, spike_right, spike_left, load_block)
    return (spike_right, spike_left, load_block)


def solution(mesh):
    in_specs = (
        P(("chain", "rows"), None),
        P(("chain", "rows"), None),
        P(("chain", "rows"), None),
        P("chain", None, None, None),
    )
    out_specs = (P(("chain", "rows"), None), P(("chain", "rows"), None), P(("chain", "rows"), None))
    return jax.shard_map(
        on_device, mesh=mesh, in_specs=in_specs, out_specs=out_specs, check_vma=False
    )
```

```python
import jax
import numpy as np
import jax.numpy as jnp
from jax import lax
from jax.experimental import pallas as pl
from jax.experimental.pallas import tpu as pltpu
from jax.sharding import PartitionSpec as P

HALF_BAND = 256
LOAD_COLS = 256
LEVELS = 3


def spread_tips(top, bottom, row_pos, count, fanouts):
    stride = count
    for fanout in fanouts:
        step = stride // fanout
        got_top = top
        got_bottom = bottom
        for k in range(1, fanout):
            offset = k * step
            pairs = [(s, s + offset) for s in range(0, count, stride)]
            pairs += [(s, s - offset) for s in range(stride - 1, count, stride)]
            sent = jnp.where(row_pos % stride == 0, top, bottom)
            got = lax.ppermute(sent, "rows", pairs)
            got_top = jnp.where(row_pos % stride == offset, got, got_top)
            got_bottom = jnp.where(row_pos % stride == stride - 1 - offset, got, got_bottom)
        top = got_top
        bottom = got_bottom
        stride = step
    return top, bottom


def row_fanouts(count):
    fanouts = []
    while count > 1:
        fanout = 4 if count % 4 == 0 else 2
        fanouts.append(fanout)
        count //= fanout
    return fanouts


def bulk_kernel(flag_ref, x_ref, v_ref, w_ref, g_ref, vo_ref, wo_ref, go_ref):
    low = flag_ref[0] == 1
    v = v_ref[...]
    w = w_ref[...]
    driver = jnp.where(low, v, w)
    d_hi = driver.astype(jnp.bfloat16)
    d_lo = (driver - d_hi.astype(jnp.float32)).astype(jnp.bfloat16)
    x = x_ref[...]
    x_hi = x.astype(jnp.bfloat16)
    x_lo = (x - x_hi.astype(jnp.float32)).astype(jnp.bfloat16)
    prod = jnp.dot(d_hi, x_hi, preferred_element_type=jnp.float32)
    prod += jnp.dot(d_hi, x_lo, preferred_element_type=jnp.float32)
    prod += jnp.dot(d_lo, x_hi, preferred_element_type=jnp.float32)
    go_ref[...] = g_ref[...] - prod[:, :LOAD_COLS]
    left_term = prod[:, LOAD_COLS:LOAD_COLS + HALF_BAND]
    right_term = prod[:, LOAD_COLS + HALF_BAND:]
    wo_ref[...] = jnp.where(low, w - left_term, -left_term)
    vo_ref[...] = jnp.where(low, -right_term, v - right_term)


def bulk_update(flag, x, v, w, g, tile=1024):
    rows = v.shape[0]
    block = pl.BlockSpec((tile, HALF_BAND), lambda i, f: (i, 0))
    out = jax.ShapeDtypeStruct((rows, HALF_BAND), jnp.float32)
    return pl.pallas_call(
        bulk_kernel,
        grid_spec=pltpu.PrefetchScalarGridSpec(
            num_scalar_prefetch=1,
            grid=(rows // tile,),
            in_specs=[pl.BlockSpec(x.shape, lambda i, f: (0, 0)), block, block, block],
            out_specs=[block, block, block],
        ),
        out_shape=[out, out, out],
    )(flag, x, v, w, g)


CORE_PLANS = (
    (((2, 0), (4, 0), (6, 0)), ((0, 1), (0, 2), (0, 3)), ((1, 0),)),
    (((0, 1), (0, 2), (0, 3)), ((2, 0), (4, 0), (6, 0)), ((7, 0),)),
)


def core_tree(top, bottom, chain_pos, row_pos, chain_count, z_count, y_count):
    row_count = z_count * y_count
    kinds = len(CORE_PLANS)

    def moved(r, off, sign):
        z, y = divmod(r, y_count)
        return ((z + sign * off[0]) % z_count) * y_count + (y + sign * off[1]) % y_count

    steps = len(CORE_PLANS[0])
    table = np.zeros((steps, 3, kinds, row_count), np.int32)
    all_pairs = []
    holders = [({0}, {row_count - 1}) for _ in CORE_PLANS]
    for step in range(steps):
        new_holders = [(set(t), set(b)) for t, b in holders]
        step_pairs = []
        for slot in range(len(CORE_PLANS[0][step])):
            pairs = []
            for kind, plan in enumerate(CORE_PLANS):
                off = plan[step][slot]
                tops, bottoms = holders[kind]
                for s in tops:
                    table[step, 2, kind, s] = 1
                    d = moved(s, off, 1)
                    table[step, 0, kind, d] = slot + 1
                    new_holders[kind][0].add(d)
                for s in bottoms:
                    d = moved(s, off, -1)
                    table[step, 1, kind, d] = slot + 1
                    new_holders[kind][1].add(d)
                for c in range(kind, chain_count, kinds):
                    pairs += [(c * row_count + s, c * row_count + moved(s, off, 1)) for s in tops]
                    pairs += [(c * row_count + s, c * row_count + moved(s, off, -1)) for s in bottoms]
            step_pairs.append(pairs)
        all_pairs.append(step_pairs)
        holders = new_holders
    mine = jnp.asarray(table.reshape(steps * 3, kinds, row_count))[:, chain_pos % kinds, row_pos]
    for step in range(steps):
        sent = jnp.where(mine[3 * step + 2] == 1, top, bottom)
        got = [lax.ppermute(sent, ("chain", "rows"), pairs) for pairs in all_pairs[step]]
        top = lax.select_n(mine[3 * step], top, *got)
        bottom = lax.select_n(mine[3 * step + 1], bottom, *got)
    return top, bottom


def on_device(right_spike, left_spike, loads, tip_inverse):
    precise = lax.Precision.HIGHEST
    band = HALF_BAND
    width = LOAD_COLS
    chain_pos = lax.axis_index("chain")
    row_pos = lax.axis_index("rows")
    chain_count = lax.axis_size("chain")
    row_count = lax.axis_size("rows")
    spike_right = right_spike
    spike_left = left_spike
    load_block = loads
    inverses = [tip_inverse[0, 0]]
    for level in range(1, LEVELS):
        half = 2**level
        place = chain_pos % (2 * half)
        lasts = list(range(half - 1, chain_count - 1, 2 * half))
        mine = tip_inverse[0, level]
        for k in range(1, half):
            pairs = [(a, a - k) for a in lasts] + [(a + 1, a + 1 + k) for a in lasts]
            got = lax.ppermute(mine, "chain", pairs)
            mine = jnp.where((place == half - 1 - k) | (place == half + k), got, mine)
        inverses.append(mine)
    first_tip = jnp.concatenate([load_block[:band], spike_right[:band]], 1)
    last_tip = jnp.concatenate([load_block[-band:], spike_left[-band:]], 1)
    if row_count == 32 and chain_count % 2 == 0:
        top, bottom = core_tree(first_tip, last_tip, chain_pos, row_pos, chain_count, 8, 4)
    else:
        top, bottom = spread_tips(first_tip, last_tip, row_pos, row_count, row_fanouts(row_count))
    inverses, top, bottom = lax.optimization_barrier((inverses, top, bottom))
    blank_block = jnp.zeros((band, band), jnp.float32)
    for level in range(LEVELS):
        half = 2**level
        place = chain_pos % (2 * half)
        side_low = place < half
        lasts = list(range(half - 1, chain_count - 1, 2 * half))
        lower_tip = bottom
        upper_tip = top
        sent = jnp.where(place == half - 1, bottom, top)
        for offset in list(range(-(half - 1), 0)) + list(range(1, half + 1)):
            pairs = [(a, a + offset) for a in lasts] + [(a + 1, a + 1 - offset) for a in lasts]
            got = lax.ppermute(sent, "chain", pairs)
            lower_tip = jnp.where(place == half - 1 + offset, got, lower_tip)
            upper_tip = jnp.where(place == half - offset, got, upper_tip)
        if level > 0:
            lower_tip, upper_tip, spike_right, spike_left, load_block = lax.optimization_barrier(
                (lower_tip, upper_tip, spike_right, spike_left, load_block)
            )
        upper_rows = jnp.concatenate([lower_tip[:, :band], lower_tip[:, band:], blank_block], 1)
        lower_rows = jnp.concatenate([upper_tip[:, :band], blank_block, upper_tip[:, band:]], 1)
        tip_rhs = jnp.concatenate([upper_rows, lower_rows], 0)
        solved = jnp.dot(inverses[level], tip_rhs, precision=precise, preferred_element_type=jnp.float32)
        if level + 1 < LEVELS:
            bottom_prod = jnp.dot(
                bottom[:, band:], solved[:, : 2 * band], precision=precise, preferred_element_type=jnp.float32
            )
            bottom = jnp.concatenate([bottom[:, :band] - bottom_prod[:, :band], -bottom_prod[:, band:]], 1)
            top_prod = jnp.dot(
                top[:, band:],
                jnp.concatenate([solved[:, :band], solved[:, 2 * band :]], 1),
                precision=precise,
                preferred_element_type=jnp.float32,
            )
            top = jnp.concatenate([top[:, :band] - top_prod[:, :band], -top_prod[:, band:]], 1)
        flag = jnp.where(side_low, 1, 0).astype(jnp.int32).reshape(1)
        spike_right, spike_left, load_block = bulk_update(flag, solved, spike_right, spike_left, load_block)
    return (spike_right, spike_left, load_block)


def solution(mesh):
    in_specs = (
        P(("chain", "rows"), None),
        P(("chain", "rows"), None),
        P(("chain", "rows"), None),
        P("chain", None, None, None),
    )
    out_specs = (P(("chain", "rows"), None), P(("chain", "rows"), None), P(("chain", "rows"), None))
    return jax.shard_map(
        on_device, mesh=mesh, in_specs=in_specs, out_specs=out_specs, check_vma=False
    )
```

```python
import jax
import numpy as np
import jax.numpy as jnp
from jax import lax
from jax.experimental import pallas as pl
from jax.experimental.pallas import tpu as pltpu
from jax.sharding import PartitionSpec as P

HALF_BAND = 256
LOAD_COLS = 256
LEVELS = 3


def spread_tips(top, bottom, row_pos, count, fanouts):
    stride = count
    for fanout in fanouts:
        step = stride // fanout
        got_top = top
        got_bottom = bottom
        for k in range(1, fanout):
            offset = k * step
            pairs = [(s, s + offset) for s in range(0, count, stride)]
            pairs += [(s, s - offset) for s in range(stride - 1, count, stride)]
            sent = jnp.where(row_pos % stride == 0, top, bottom)
            got = lax.ppermute(sent, "rows", pairs)
            got_top = jnp.where(row_pos % stride == offset, got, got_top)
            got_bottom = jnp.where(row_pos % stride == stride - 1 - offset, got, got_bottom)
        top = got_top
        bottom = got_bottom
        stride = step
    return top, bottom


def row_fanouts(count):
    fanouts = []
    while count > 1:
        fanout = 4 if count % 4 == 0 else 2
        fanouts.append(fanout)
        count //= fanout
    return fanouts


def bulk_kernel(flag_ref, x_ref, v_ref, w_ref, g_ref, vo_ref, wo_ref, go_ref):
    low = flag_ref[0] == 1
    v = v_ref[...]
    w = w_ref[...]
    driver = jnp.where(low, v, w)
    d_hi = driver.astype(jnp.bfloat16)
    d_lo = (driver - d_hi.astype(jnp.float32)).astype(jnp.bfloat16)
    x = x_ref[...]
    x_hi = x.astype(jnp.bfloat16)
    x_lo = (x - x_hi.astype(jnp.float32)).astype(jnp.bfloat16)
    prod = jnp.dot(d_hi, x_hi, preferred_element_type=jnp.float32)
    prod += jnp.dot(d_hi, x_lo, preferred_element_type=jnp.float32)
    prod += jnp.dot(d_lo, x_hi, preferred_element_type=jnp.float32)
    go_ref[...] = g_ref[...] - prod[:, :LOAD_COLS]
    left_term = prod[:, LOAD_COLS:LOAD_COLS + HALF_BAND]
    right_term = prod[:, LOAD_COLS + HALF_BAND:]
    wo_ref[...] = jnp.where(low, w - left_term, -left_term)
    vo_ref[...] = jnp.where(low, -right_term, v - right_term)


def bulk_update(flag, x, v, w, g, tile=1024):
    rows = v.shape[0]
    block = pl.BlockSpec((tile, HALF_BAND), lambda i, f: (i, 0))
    out = jax.ShapeDtypeStruct((rows, HALF_BAND), jnp.float32)
    return pl.pallas_call(
        bulk_kernel,
        grid_spec=pltpu.PrefetchScalarGridSpec(
            num_scalar_prefetch=1,
            grid=(rows // tile,),
            in_specs=[pl.BlockSpec(x.shape, lambda i, f: (0, 0)), block, block, block],
            out_specs=[block, block, block],
        ),
        out_shape=[out, out, out],
    )(flag, x, v, w, g)


CORE_PLANS = (
    (((2, 0), (4, 0), (6, 0)), ((0, 1), (0, 2), (0, 3)), ((1, 0),)),
    (((0, 1), (0, 2), (0, 3)), ((2, 0), (4, 0), (6, 0)), ((7, 0),)),
)


def core_tree(top, bottom, chain_pos, row_pos, chain_count, z_count, y_count, rider):
    row_count = z_count * y_count
    kinds = len(CORE_PLANS)

    def moved(r, off, sign):
        z, y = divmod(r, y_count)
        return ((z + sign * off[0]) % z_count) * y_count + (y + sign * off[1]) % y_count

    steps = len(CORE_PLANS[0])
    table = np.zeros((steps, 3, kinds, row_count), np.int32)
    all_pairs = []
    holders = [({0}, {row_count - 1}) for _ in CORE_PLANS]
    for step in range(steps):
        new_holders = [(set(t), set(b)) for t, b in holders]
        step_pairs = []
        for slot in range(len(CORE_PLANS[0][step])):
            pairs = []
            for kind, plan in enumerate(CORE_PLANS):
                off = plan[step][slot]
                tops, bottoms = holders[kind]
                for s in tops:
                    table[step, 2, kind, s] = 1
                    d = moved(s, off, 1)
                    table[step, 0, kind, d] = slot + 1
                    new_holders[kind][0].add(d)
                for s in bottoms:
                    d = moved(s, off, -1)
                    table[step, 1, kind, d] = slot + 1
                    new_holders[kind][1].add(d)
                for c in range(kind, chain_count, kinds):
                    pairs += [(c * row_count + s, c * row_count + moved(s, off, 1)) for s in tops]
                    pairs += [(c * row_count + s, c * row_count + moved(s, off, -1)) for s in bottoms]
            step_pairs.append(pairs)
        all_pairs.append(step_pairs)
        holders = new_holders
    mine = jnp.asarray(table.reshape(steps * 3, kinds, row_count))[:, chain_pos % kinds, row_pos]
    for step in range(steps):
        sent = jnp.where(mine[3 * step + 2] == 1, top, bottom)
        got = [lax.ppermute(sent, ("chain", "rows"), pairs) for pairs in all_pairs[step]]
        top = lax.select_n(mine[3 * step], top, *got)
        bottom = lax.select_n(mine[3 * step + 1], bottom, *got)
        if step == 0:
            rider, top, bottom = lax.optimization_barrier((rider, top, bottom))
    return top, bottom, rider


def on_device(right_spike, left_spike, loads, tip_inverse):
    precise = lax.Precision.HIGHEST
    band = HALF_BAND
    width = LOAD_COLS
    chain_pos = lax.axis_index("chain")
    row_pos = lax.axis_index("rows")
    chain_count = lax.axis_size("chain")
    row_count = lax.axis_size("rows")
    spike_right = right_spike
    spike_left = left_spike
    load_block = loads
    first_tip = jnp.concatenate([load_block[:band], spike_right[:band]], 1)
    last_tip = jnp.concatenate([load_block[-band:], spike_left[-band:]], 1)
    if row_count == 32 and chain_count % 2 == 0:
        top, bottom, tip_inverse = core_tree(first_tip, last_tip, chain_pos, row_pos, chain_count, 8, 4, tip_inverse)
    else:
        top, bottom = spread_tips(first_tip, last_tip, row_pos, row_count, row_fanouts(row_count))
    inverses = [tip_inverse[0, 0]]
    for level in range(1, LEVELS):
        half = 2**level
        place = chain_pos % (2 * half)
        lasts = list(range(half - 1, chain_count - 1, 2 * half))
        mine = tip_inverse[0, level]
        for k in range(1, half):
            pairs = [(a, a - k) for a in lasts] + [(a + 1, a + 1 + k) for a in lasts]
            got = lax.ppermute(mine, "chain", pairs)
            mine = jnp.where((place == half - 1 - k) | (place == half + k), got, mine)
        inverses.append(mine)
    inverses, top, bottom = lax.optimization_barrier((inverses, top, bottom))
    blank_block = jnp.zeros((band, band), jnp.float32)
    for level in range(LEVELS):
        half = 2**level
        place = chain_pos % (2 * half)
        side_low = place < half
        lasts = list(range(half - 1, chain_count - 1, 2 * half))
        lower_tip = bottom
        upper_tip = top
        sent = jnp.where(place == half - 1, bottom, top)
        for offset in list(range(-(half - 1), 0)) + list(range(1, half + 1)):
            pairs = [(a, a + offset) for a in lasts] + [(a + 1, a + 1 - offset) for a in lasts]
            got = lax.ppermute(sent, "chain", pairs)
            lower_tip = jnp.where(place == half - 1 + offset, got, lower_tip)
            upper_tip = jnp.where(place == half - offset, got, upper_tip)
        if level > 0:
            lower_tip, upper_tip, spike_right, spike_left, load_block = lax.optimization_barrier(
                (lower_tip, upper_tip, spike_right, spike_left, load_block)
            )
        upper_rows = jnp.concatenate([lower_tip[:, :band], lower_tip[:, band:], blank_block], 1)
        lower_rows = jnp.concatenate([upper_tip[:, :band], blank_block, upper_tip[:, band:]], 1)
        tip_rhs = jnp.concatenate([upper_rows, lower_rows], 0)
        solved = jnp.dot(inverses[level], tip_rhs, precision=precise, preferred_element_type=jnp.float32)
        if level + 1 < LEVELS:
            bottom_prod = jnp.dot(
                bottom[:, band:], solved[:, : 2 * band], precision=precise, preferred_element_type=jnp.float32
            )
            bottom = jnp.concatenate([bottom[:, :band] - bottom_prod[:, :band], -bottom_prod[:, band:]], 1)
            top_prod = jnp.dot(
                top[:, band:],
                jnp.concatenate([solved[:, :band], solved[:, 2 * band :]], 1),
                precision=precise,
                preferred_element_type=jnp.float32,
            )
            top = jnp.concatenate([top[:, :band] - top_prod[:, :band], -top_prod[:, band:]], 1)
        flag = jnp.where(side_low, 1, 0).astype(jnp.int32).reshape(1)
        spike_right, spike_left, load_block = bulk_update(flag, solved, spike_right, spike_left, load_block)
    return (spike_right, spike_left, load_block)


def solution(mesh):
    in_specs = (
        P(("chain", "rows"), None),
        P(("chain", "rows"), None),
        P(("chain", "rows"), None),
        P("chain", None, None, None),
    )
    out_specs = (P(("chain", "rows"), None), P(("chain", "rows"), None), P(("chain", "rows"), None))
    return jax.shard_map(
        on_device, mesh=mesh, in_specs=in_specs, out_specs=out_specs, check_vma=False
    )
```

```python
import jax
import numpy as np
import jax.numpy as jnp
from jax import lax
from jax.experimental import pallas as pl
from jax.experimental.pallas import tpu as pltpu
from jax.sharding import PartitionSpec as P

HALF_BAND = 256
LOAD_COLS = 256
LEVELS = 3


def spread_tips(top, bottom, row_pos, count, fanouts):
    stride = count
    for fanout in fanouts:
        step = stride // fanout
        got_top = top
        got_bottom = bottom
        for k in range(1, fanout):
            offset = k * step
            pairs = [(s, s + offset) for s in range(0, count, stride)]
            pairs += [(s, s - offset) for s in range(stride - 1, count, stride)]
            sent = jnp.where(row_pos % stride == 0, top, bottom)
            got = lax.ppermute(sent, "rows", pairs)
            got_top = jnp.where(row_pos % stride == offset, got, got_top)
            got_bottom = jnp.where(row_pos % stride == stride - 1 - offset, got, got_bottom)
        top = got_top
        bottom = got_bottom
        stride = step
    return top, bottom


def row_fanouts(count):
    fanouts = []
    while count > 1:
        fanout = 4 if count % 4 == 0 else 2
        fanouts.append(fanout)
        count //= fanout
    return fanouts


def bulk_kernel(flag_ref, x_ref, v_ref, w_ref, g_ref, vo_ref, wo_ref, go_ref):
    low = flag_ref[0] == 1
    v = v_ref[...]
    w = w_ref[...]
    driver = jnp.where(low, v, w)
    d_hi = driver.astype(jnp.bfloat16)
    d_lo = (driver - d_hi.astype(jnp.float32)).astype(jnp.bfloat16)
    x = x_ref[...]
    x_hi = x.astype(jnp.bfloat16)
    x_lo = (x - x_hi.astype(jnp.float32)).astype(jnp.bfloat16)
    prod = jnp.dot(d_hi, x_hi, preferred_element_type=jnp.float32)
    prod += jnp.dot(d_hi, x_lo, preferred_element_type=jnp.float32)
    prod += jnp.dot(d_lo, x_hi, preferred_element_type=jnp.float32)
    go_ref[...] = g_ref[...] - prod[:, :LOAD_COLS]
    left_term = prod[:, LOAD_COLS:LOAD_COLS + HALF_BAND]
    right_term = prod[:, LOAD_COLS + HALF_BAND:]
    wo_ref[...] = jnp.where(low, w - left_term, -left_term)
    vo_ref[...] = jnp.where(low, -right_term, v - right_term)


def bulk_update(flag, x, v, w, g, tile=1024):
    rows = v.shape[0]
    block = pl.BlockSpec((tile, HALF_BAND), lambda i, f: (i, 0))
    out = jax.ShapeDtypeStruct((rows, HALF_BAND), jnp.float32)
    return pl.pallas_call(
        bulk_kernel,
        grid_spec=pltpu.PrefetchScalarGridSpec(
            num_scalar_prefetch=1,
            grid=(rows // tile,),
            in_specs=[pl.BlockSpec(x.shape, lambda i, f: (0, 0)), block, block, block],
            out_specs=[block, block, block],
        ),
        out_shape=[out, out, out],
    )(flag, x, v, w, g)


CORE_PLANS = (
    (((2, 0), (4, 0), (6, 0)), ((0, 1), (0, 2), (0, 3)), ((1, 0),)),
    (((0, 1), (0, 2), (0, 3)), ((2, 0), (4, 0), (6, 0)), ((7, 0),)),
)


def core_tree(top, bottom, chain_pos, row_pos, chain_count, z_count, y_count):
    row_count = z_count * y_count
    kinds = len(CORE_PLANS)

    def moved(r, off, sign):
        z, y = divmod(r, y_count)
        return ((z + sign * off[0]) % z_count) * y_count + (y + sign * off[1]) % y_count

    steps = len(CORE_PLANS[0])
    table = np.zeros((steps, 3, kinds, row_count), np.int32)
    all_pairs = []
    holders = [({0}, {row_count - 1}) for _ in CORE_PLANS]
    for step in range(steps):
        new_holders = [(set(t), set(b)) for t, b in holders]
        step_pairs = []
        for slot in range(len(CORE_PLANS[0][step])):
            pairs = []
            for kind, plan in enumerate(CORE_PLANS):
                off = plan[step][slot]
                tops, bottoms = holders[kind]
                for s in tops:
                    table[step, 2, kind, s] = 1
                    d = moved(s, off, 1)
                    table[step, 0, kind, d] = slot + 1
                    new_holders[kind][0].add(d)
                for s in bottoms:
                    d = moved(s, off, -1)
                    table[step, 1, kind, d] = slot + 1
                    new_holders[kind][1].add(d)
                for c in range(kind, chain_count, kinds):
                    pairs += [(c * row_count + s, c * row_count + moved(s, off, 1)) for s in tops]
                    pairs += [(c * row_count + s, c * row_count + moved(s, off, -1)) for s in bottoms]
            step_pairs.append(pairs)
        all_pairs.append(step_pairs)
        holders = new_holders
    mine = jnp.asarray(table.reshape(steps * 3, kinds, row_count))[:, chain_pos % kinds, row_pos]
    for step in range(steps):
        sent = jnp.where(mine[3 * step + 2] == 1, top, bottom)
        got = [lax.ppermute(sent, ("chain", "rows"), pairs) for pairs in all_pairs[step]]
        top = lax.select_n(mine[3 * step], top, *got)
        bottom = lax.select_n(mine[3 * step + 1], bottom, *got)
    return top, bottom


def on_device(right_spike, left_spike, loads, tip_inverse):
    precise = lax.Precision.HIGHEST
    band = HALF_BAND
    width = LOAD_COLS
    chain_pos = lax.axis_index("chain")
    row_pos = lax.axis_index("rows")
    chain_count = lax.axis_size("chain")
    row_count = lax.axis_size("rows")
    spike_right = right_spike
    spike_left = left_spike
    load_block = loads
    inverses = [tip_inverse[0, 0]]
    for level in range(1, LEVELS):
        half = 2**level
        place = chain_pos % (2 * half)
        lasts = list(range(half - 1, chain_count - 1, 2 * half))
        mine = tip_inverse[0, level]
        for k in range(1, half):
            pairs = [(a, a - k) for a in lasts] + [(a + 1, a + 1 + k) for a in lasts]
            got = lax.ppermute(mine, "chain", pairs)
            mine = jnp.where((place == half - 1 - k) | (place == half + k), got, mine)
        inverses.append(mine)
    first_tip = jnp.concatenate([load_block[:band], spike_right[:band]], 1)
    last_tip = jnp.concatenate([load_block[-band:], spike_left[-band:]], 1)
    if row_count == 32 and chain_count % 2 == 0:
        top, bottom = core_tree(first_tip, last_tip, chain_pos, row_pos, chain_count, 8, 4)
    else:
        top, bottom = spread_tips(first_tip, last_tip, row_pos, row_count, row_fanouts(row_count))
    inverses, top, bottom = lax.optimization_barrier((inverses, top, bottom))
    for level in range(LEVELS):
        half = 2**level
        place = chain_pos % (2 * half)
        side_low = place < half
        lasts = list(range(half - 1, chain_count - 1, 2 * half))
        lower_tip = bottom
        upper_tip = top
        sent = jnp.where(place == half - 1, bottom, top)
        for offset in list(range(-(half - 1), 0)) + list(range(1, half + 1)):
            pairs = [(a, a + offset) for a in lasts] + [(a + 1, a + 1 - offset) for a in lasts]
            got = lax.ppermute(sent, "chain", pairs)
            lower_tip = jnp.where(place == half - 1 + offset, got, lower_tip)
            upper_tip = jnp.where(place == half - offset, got, upper_tip)
        if level > 0:
            lower_tip, upper_tip, spike_right, spike_left, load_block = lax.optimization_barrier(
                (lower_tip, upper_tip, spike_right, spike_left, load_block)
            )
        inverse_low = inverses[level][:, :band]
        inverse_up = inverses[level][:, band:]
        solved_load = jnp.dot(
            inverse_low, lower_tip[:, :band], precision=precise, preferred_element_type=jnp.float32
        ) + jnp.dot(inverse_up, upper_tip[:, :band], precision=precise, preferred_element_type=jnp.float32)
        solved_left = jnp.dot(inverse_low, lower_tip[:, band:], precision=precise, preferred_element_type=jnp.float32)
        solved_right = jnp.dot(inverse_up, upper_tip[:, band:], precision=precise, preferred_element_type=jnp.float32)
        solved = jnp.concatenate([solved_load, solved_left, solved_right], 1)
        if level + 1 < LEVELS:
            bottom_prod = jnp.dot(
                bottom[:, band:], solved[:, : 2 * band], precision=precise, preferred_element_type=jnp.float32
            )
            bottom = jnp.concatenate([bottom[:, :band] - bottom_prod[:, :band], -bottom_prod[:, band:]], 1)
            top_prod = jnp.dot(
                top[:, band:],
                jnp.concatenate([solved[:, :band], solved[:, 2 * band :]], 1),
                precision=precise,
                preferred_element_type=jnp.float32,
            )
            top = jnp.concatenate([top[:, :band] - top_prod[:, :band], -top_prod[:, band:]], 1)
        flag = jnp.where(side_low, 1, 0).astype(jnp.int32).reshape(1)
        spike_right, spike_left, load_block = bulk_update(flag, solved, spike_right, spike_left, load_block)
    return (spike_right, spike_left, load_block)


def solution(mesh):
    in_specs = (
        P(("chain", "rows"), None),
        P(("chain", "rows"), None),
        P(("chain", "rows"), None),
        P("chain", None, None, None),
    )
    out_specs = (P(("chain", "rows"), None), P(("chain", "rows"), None), P(("chain", "rows"), None))
    return jax.shard_map(
        on_device, mesh=mesh, in_specs=in_specs, out_specs=out_specs, check_vma=False
    )
```

```python
import jax
import numpy as np
import jax.numpy as jnp
from jax import lax
from jax.experimental import pallas as pl
from jax.experimental.pallas import tpu as pltpu
from jax.sharding import PartitionSpec as P

HALF_BAND = 256
LOAD_COLS = 256
LEVELS = 3


def spread_tips(top, bottom, row_pos, count, fanouts):
    stride = count
    for fanout in fanouts:
        step = stride // fanout
        got_top = top
        got_bottom = bottom
        for k in range(1, fanout):
            offset = k * step
            pairs = [(s, s + offset) for s in range(0, count, stride)]
            pairs += [(s, s - offset) for s in range(stride - 1, count, stride)]
            sent = jnp.where(row_pos % stride == 0, top, bottom)
            got = lax.ppermute(sent, "rows", pairs)
            got_top = jnp.where(row_pos % stride == offset, got, got_top)
            got_bottom = jnp.where(row_pos % stride == stride - 1 - offset, got, got_bottom)
        top = got_top
        bottom = got_bottom
        stride = step
    return top, bottom


def row_fanouts(count):
    fanouts = []
    while count > 1:
        fanout = 4 if count % 4 == 0 else 2
        fanouts.append(fanout)
        count //= fanout
    return fanouts


def bulk_kernel(flag_ref, x_ref, v_ref, w_ref, g_ref, vo_ref, wo_ref, go_ref):
    low = flag_ref[0] == 1
    v = v_ref[...]
    w = w_ref[...]
    driver = jnp.where(low, v, w)
    d_hi = driver.astype(jnp.bfloat16)
    d_lo = (driver - d_hi.astype(jnp.float32)).astype(jnp.bfloat16)
    x = x_ref[...]
    x_hi = x.astype(jnp.bfloat16)
    x_lo = (x - x_hi.astype(jnp.float32)).astype(jnp.bfloat16)
    prod = jnp.dot(d_hi, x_hi, preferred_element_type=jnp.float32)
    prod += jnp.dot(d_hi, x_lo, preferred_element_type=jnp.float32)
    prod += jnp.dot(d_lo, x_hi, preferred_element_type=jnp.float32)
    go_ref[...] = g_ref[...] - prod[:, :LOAD_COLS]
    left_term = prod[:, LOAD_COLS:LOAD_COLS + HALF_BAND]
    right_term = prod[:, LOAD_COLS + HALF_BAND:]
    wo_ref[...] = jnp.where(low, w - left_term, -left_term)
    vo_ref[...] = jnp.where(low, -right_term, v - right_term)


def bulk_update(flag, x, v, w, g, tile=1024):
    rows = v.shape[0]
    block = pl.BlockSpec((tile, HALF_BAND), lambda i, f: (i, 0))
    out = jax.ShapeDtypeStruct((rows, HALF_BAND), jnp.float32)
    return pl.pallas_call(
        bulk_kernel,
        grid_spec=pltpu.PrefetchScalarGridSpec(
            num_scalar_prefetch=1,
            grid=(rows // tile,),
            in_specs=[pl.BlockSpec(x.shape, lambda i, f: (0, 0)), block, block, block],
            out_specs=[block, block, block],
        ),
        out_shape=[out, out, out],
    )(flag, x, v, w, g)


CORE_PLANS = (
    (((2, 0), (4, 0), (6, 0)), ((0, 1), (0, 2), (0, 3)), ((1, 0),)),
    (((0, 1), (0, 2), (0, 3)), ((2, 0), (4, 0), (6, 0)), ((7, 0),)),
)


def core_tree(top, bottom, chain_pos, row_pos, chain_count, z_count, y_count):
    row_count = z_count * y_count
    kinds = len(CORE_PLANS)

    def moved(r, off, sign):
        z, y = divmod(r, y_count)
        return ((z + sign * off[0]) % z_count) * y_count + (y + sign * off[1]) % y_count

    steps = len(CORE_PLANS[0])
    table = np.zeros((steps, 3, kinds, row_count), np.int32)
    all_pairs = []
    holders = [({0}, {row_count - 1}) for _ in CORE_PLANS]
    for step in range(steps):
        new_holders = [(set(t), set(b)) for t, b in holders]
        step_pairs = []
        for slot in range(len(CORE_PLANS[0][step])):
            pairs = []
            for kind, plan in enumerate(CORE_PLANS):
                off = plan[step][slot]
                tops, bottoms = holders[kind]
                for s in tops:
                    table[step, 2, kind, s] = 1
                    d = moved(s, off, 1)
                    table[step, 0, kind, d] = slot + 1
                    new_holders[kind][0].add(d)
                for s in bottoms:
                    d = moved(s, off, -1)
                    table[step, 1, kind, d] = slot + 1
                    new_holders[kind][1].add(d)
                for c in range(kind, chain_count, kinds):
                    pairs += [(c * row_count + s, c * row_count + moved(s, off, 1)) for s in tops]
                    pairs += [(c * row_count + s, c * row_count + moved(s, off, -1)) for s in bottoms]
            step_pairs.append(pairs)
        all_pairs.append(step_pairs)
        holders = new_holders
    mine = jnp.asarray(table.reshape(steps * 3, kinds, row_count))[:, chain_pos % kinds, row_pos]
    for step in range(steps):
        sent = jnp.where(mine[3 * step + 2] == 1, top, bottom)
        got = [lax.ppermute(sent, ("chain", "rows"), pairs) for pairs in all_pairs[step]]
        top = lax.select_n(mine[3 * step], top, *got)
        bottom = lax.select_n(mine[3 * step + 1], bottom, *got)
    return top, bottom


def on_device(right_spike, left_spike, loads, tip_inverse):
    precise = lax.Precision.HIGHEST
    band = HALF_BAND
    width = LOAD_COLS
    chain_pos = lax.axis_index("chain")
    row_pos = lax.axis_index("rows")
    chain_count = lax.axis_size("chain")
    row_count = lax.axis_size("rows")
    spike_right = right_spike
    spike_left = left_spike
    load_block = loads
    inverses = [tip_inverse[0, 0]]
    for level in range(1, LEVELS):
        half = 2**level
        place = chain_pos % (2 * half)
        lasts = list(range(half - 1, chain_count - 1, 2 * half))
        mine = tip_inverse[0, level]
        for k in range(1, half):
            pairs = [(a, a - k) for a in lasts] + [(a + 1, a + 1 + k) for a in lasts]
            got = lax.ppermute(mine, "chain", pairs)
            mine = jnp.where((place == half - 1 - k) | (place == half + k), got, mine)
        inverses.append(mine)
    first_tip = jnp.concatenate([load_block[:band], spike_right[:band]], 1)
    last_tip = jnp.concatenate([load_block[-band:], spike_left[-band:]], 1)
    if row_count == 32 and chain_count % 2 == 0:
        top, bottom = core_tree(first_tip, last_tip, chain_pos, row_pos, chain_count, 8, 4)
    else:
        top, bottom = spread_tips(first_tip, last_tip, row_pos, row_count, row_fanouts(row_count))
    inverses, top, bottom = lax.optimization_barrier((inverses, top, bottom))
    blank_block = jnp.zeros((band, band), jnp.float32)
    for level in range(LEVELS):
        half = 2**level
        place = chain_pos % (2 * half)
        side_low = place < half
        lasts = list(range(half - 1, chain_count - 1, 2 * half))
        lower_tip = bottom
        upper_tip = top
        sent = jnp.where(place == half - 1, bottom, top)
        for offset in list(range(-(half - 1), 0)) + list(range(1, half + 1)):
            pairs = [(a, a + offset) for a in lasts] + [(a + 1, a + 1 - offset) for a in lasts]
            got = lax.ppermute(sent, "chain", pairs)
            lower_tip = jnp.where(place == half - 1 + offset, got, lower_tip)
            upper_tip = jnp.where(place == half - offset, got, upper_tip)
        if level > 0:
            lower_tip, upper_tip, spike_right, spike_left, load_block = lax.optimization_barrier(
                (lower_tip, upper_tip, spike_right, spike_left, load_block)
            )
        upper_rows = jnp.concatenate([lower_tip[:, :band], lower_tip[:, band:], blank_block], 1)
        lower_rows = jnp.concatenate([upper_tip[:, :band], blank_block, upper_tip[:, band:]], 1)
        tip_rhs = jnp.concatenate([upper_rows, lower_rows], 0)
        solved = jnp.dot(inverses[level], tip_rhs, precision=precise, preferred_element_type=jnp.float32)
        if level + 1 < LEVELS:
            tip = jnp.where(side_low, top, bottom)
            cols = jnp.concatenate(
                [solved[:, :band], jnp.where(side_low, solved[:, 2 * band :], solved[:, band : 2 * band])], 1
            )
            tip_prod = jnp.dot(tip[:, band:], cols, precision=precise, preferred_element_type=jnp.float32)
            tip = jnp.concatenate([tip[:, :band] - tip_prod[:, :band], -tip_prod[:, band:]], 1)
            top = jnp.where(side_low, tip, top)
            bottom = jnp.where(side_low, bottom, tip)
        flag = jnp.where(side_low, 1, 0).astype(jnp.int32).reshape(1)
        spike_right, spike_left, load_block = bulk_update(flag, solved, spike_right, spike_left, load_block)
    return (spike_right, spike_left, load_block)


def solution(mesh):
    in_specs = (
        P(("chain", "rows"), None),
        P(("chain", "rows"), None),
        P(("chain", "rows"), None),
        P("chain", None, None, None),
    )
    out_specs = (P(("chain", "rows"), None), P(("chain", "rows"), None), P(("chain", "rows"), None))
    return jax.shard_map(
        on_device, mesh=mesh, in_specs=in_specs, out_specs=out_specs, check_vma=False
    )
```
